128 devices in a mesh: seq: 32 (over x, z, core), mp: 4 (over y).
Axes of the slice: x: 4, y: 4, z: 4, core: 2. Of those that a mesh axis runs over, the one named last changes fastest.
Arguments:
- hidden: bfloat16 [16384, 4096], P('seq', 'mp'), may hold values from -6 to 6
- w_zx: bfloat16 [4096, 2, 4096], P(None, None, 'mp'), may hold values from -0.09375 to 0.09375
- w_bc: bfloat16 [4096, 2, 512], P(None, None, 'mp'), may hold values from -0.09375 to 0.09375
- w_dt: bfloat16 [4096, 64], P(None, 'mp'), may hold values from -0.09375 to 0.09375
- conv_x: float32 [4, 4096], P(None, 'mp'), may hold values from -3 to 3
- conv_x_bias: float32 [4096], P('mp'), may hold values from -3 to 3
- conv_bc: float32 [4, 2, 512], P(None, None, 'mp'), may hold values from -3 to 3
- conv_bc_bias: float32 [2, 512], P(None, 'mp'), may hold values from -3 to 3
- a_log: float32 [64], P('mp'), may hold values from -9.5 to -0.5
- dt_bias: float32 [64], P('mp'), may hold values from -4 to -1
- d_skip: float32 [64], P('mp'), may hold values from 0.5 to 4
- norm_gain: float32 [4096], P('mp'), may hold values from 0.4 to 1.6
- state_bank: float32 [2, 64, 64, 128], P(None, 'mp'), may hold values from -2 to 2
- conv_bank_x: bfloat16 [2, 3, 4096], P(None, None, 'mp'), may hold values from -5 to 5
- conv_bank_bc: bfloat16 [2, 3, 2, 512], P(None, None, None, 'mp'), may hold values from -5 to 5
- prompt_blocks: int32 [9], replicated, may hold values from 1 to 48, 64 in all
- prompt_order: int32 [9], replicated, may hold values from 0 to 8, each once
- resume_slot: int32 [9], replicated, may hold values from 0 to 2
Outputs:
- mixed: bfloat16 [16384, 4096], P('seq', 'mp')
The draws below stay inside these ranges and needn't reach their ends.
Inputs may be any that keep to these rules, and one draw needn't show every extreme that they name: `prompt_blocks`: blocks of each prompt; they sum to 64 and the longest is exactly 48. `prompt_order`: A permutation of the prompts. `resume_slot`: 2 means a fresh start from zero state and zero convolution rows.
All inputs are finite; a program needn't handle non-finite values.
Results may differ from the reference program's by a relative error of at most 0.0068.
Values may be sent and summed in bfloat16 or wider, within the bound.
No kernel may reach another device: no remote copies, remote signals or barrier semaphores. Data moves between devices by JAX's collectives and lax.ppermute only.
A program may use at most 192 MiB of HBM per device.

```python
import math
import jax
import jax.numpy as jnp
import numpy as np
from jax import lax

WIDTH = 4096
HEADS = 64
HEAD_DIM = 64
GROUPS = 4
STATE = 128
BLOCK = 256
KERNEL = 4
BLOCKS_DEV = 2
BANK = 2
INNER = 4096
GROUP_STATE = 512
NBLOCKS = 64
TOKENS = 16384
PROMPTS = 9
LONGEST = 48
N_SEQ = 32


def draw_a_log(key, part):
    key_slow = jax.random.fold_in(key, 11)
    key_fast = jax.random.fold_in(key, 12)
    key_pick = jax.random.fold_in(key, 13)
    slow = jax.random.uniform(key_slow, (HEADS,), jnp.float32, -9.5, -3.5)
    fast = jax.random.uniform(key_fast, (HEADS,), jnp.float32, -2.0, -0.5)
    chosen = jax.random.randint(key_pick, (HEADS // 8, 1), 0, 8)
    marked = (jnp.arange(8, dtype=jnp.int32)[None, :] == chosen).reshape(HEADS)
    return jnp.where(marked, fast, slow)


def with_ends(entries, rng, low, top_value):
    longest = entries.shape.index(max(entries.shape))
    spots = []
    for shift in (0, 1):
        where = [jax.random.randint(jax.random.fold_in(rng, axis), (), 0, length) for axis, length in enumerate(entries.shape)]
        where[longest] = (where[longest] + shift) % entries.shape[longest]
        spots.append(tuple(where))
    return entries.at[spots[0]].set(low).at[spots[1]].set(top_value)


def block_scale(own_key, extent, pieces, low, top_value):
    loudness, own = 1.0, jax.random.fold_in(own_key, 6)
    for position, shards_of in pieces:
        heights = jnp.exp(jax.random.uniform(jax.random.fold_in(own, position), (shards_of,), jnp.float32, low / len(pieces), top_value / len(pieces)))
        loudness = loudness * jnp.repeat(heights, extent[position] // shards_of).reshape([-1 if axis == position else 1 for axis in range(len(extent))])
    return loudness


def length_profile(amount, total, limit, slope):
    weights = [(1 << 20) // math.isqrt(standing ** slope) + 1 for standing in range(2, amount + 1)]
    rest, given = total - limit - (amount - 1), [1] * (amount - 1)
    while rest > 0:
        candidates = [i for i in range(amount - 1) if given[i] < limit]
        mass, budget = sum([weights[i] for i in candidates]), rest
        for i in candidates:
            more = min(limit - given[i], max(1, budget * weights[i] // mass), rest)
            given[i] = given[i] + more
            rest = rest - more
    return np.array([limit] + given)


def uneven_parts(stream_key, amount, total, bound, lean):
    if amount == 2:
        one = jax.random.randint(stream_key, (), max(1, total - bound), min(bound, total - 1) + 1)
        return jnp.stack([one, total - one])
    sizes = jnp.asarray(length_profile(amount, total, bound, lean), jnp.int32)
    twos = (amount - 1) // 2
    source_of, receiver = sizes[1:1 + 2 * twos:2], sizes[2:2 + 2 * twos:2]
    slack = jnp.minimum(source_of - 1, bound - receiver)
    moved = jax.random.randint(jax.random.fold_in(stream_key, 1), (twos,), 0, 1 << 20) % (slack + 1)
    sizes = sizes.at[1:1 + 2 * twos:2].set(source_of - moved).at[2:2 + 2 * twos:2].set(receiver + moved)
    return sizes[jax.random.permutation(jax.random.fold_in(stream_key, 2), amount)]


def gaussian(key, shape, width, reach, cuts=(), held_as=jnp.bfloat16):
    gain = block_scale(key, shape, cuts, -0.22, 0.18) if cuts else 1.0
    array = jax.random.normal(key, shape, jnp.float32) * width * gain
    return jnp.minimum(jnp.maximum(array, -reach), reach).astype(held_as)


def setup_inputs(seed: int = 0) -> dict:
    keys = jax.random.split(jax.random.key(seed), 19)
    hidden = gaussian(keys[0], (TOKENS, WIDTH), 1.0, 6.0, ((0, 32), (1, 4)))
    w_zx = gaussian(keys[1], (WIDTH, 2, INNER), WIDTH ** -0.5, 0.09375, ((2, 4),))
    w_bc = gaussian(keys[2], (WIDTH, 2, GROUP_STATE), WIDTH ** -0.5, 0.09375, ((2, 4),))
    w_dt = gaussian(keys[3], (WIDTH, HEADS), WIDTH ** -0.5, 0.09375, ((1, 4),))
    conv_x = gaussian(keys[4], (KERNEL, INNER), KERNEL ** -0.5, 3.0, ((1, 4),), jnp.float32)
    conv_x_bias = gaussian(keys[5], (INNER,), 0.5, 3.0, ((0, 4),), jnp.float32)
    conv_bc = gaussian(keys[6], (KERNEL, 2, GROUP_STATE), KERNEL ** -0.5, 3.0, ((2, 4),), jnp.float32)
    conv_bc_bias = gaussian(keys[7], (2, GROUP_STATE), 0.5, 3.0, ((1, 4),), jnp.float32)
    a_log = draw_a_log(jax.random.fold_in(keys[18], 71), 0)
    dt_bias = jnp.clip(-4.0 + 3.0 * jax.random.uniform(keys[9], (HEADS,), jnp.float32) ** block_scale(keys[9], (HEADS,), ((0, 4),), -0.2, 0.2), -4.0, -1.0)
    d_skip = jnp.clip(0.5 + 3.5 * jax.random.uniform(keys[10], (HEADS,), jnp.float32) ** block_scale(keys[10], (HEADS,), ((0, 4),), -0.2, 0.2), 0.5, 4.0)
    norm_gain = jnp.clip(1.0 + 0.12 * jax.random.normal(keys[11], (INNER,), jnp.float32), 0.4, 1.6)
    state_bank = gaussian(keys[12], (BANK, HEADS, HEAD_DIM, STATE), 0.3, 2.0, ((1, 4),), jnp.float32)
    conv_bank_x = gaussian(keys[13], (BANK, KERNEL - 1, INNER), 1.0, 5.0, ((2, 4),))
    conv_bank_bc = gaussian(keys[14], (BANK, KERNEL - 1, 2, GROUP_STATE), 1.0, 5.0, ((3, 4),))
    prompt_blocks = uneven_parts(keys[15], PROMPTS, NBLOCKS, LONGEST, 2).astype(jnp.int32)
    prompt_order = jax.random.permutation(keys[16], PROMPTS).astype(jnp.int32)
    resume_slot = with_ends(jax.random.randint(keys[17], (PROMPTS,), 0, BANK + 1), jax.random.fold_in(keys[17], 1), 0, BANK).astype(jnp.int32)
    return dict(hidden=hidden, w_zx=w_zx, w_bc=w_bc, w_dt=w_dt, conv_x=conv_x, conv_x_bias=conv_x_bias, conv_bc=conv_bc, conv_bc_bias=conv_bc_bias, a_log=a_log, dt_bias=dt_bias, d_skip=d_skip, norm_gain=norm_gain, state_bank=state_bank, conv_bank_x=conv_bank_x, conv_bank_bc=conv_bank_bc, prompt_blocks=prompt_blocks, prompt_order=prompt_order, resume_slot=resume_slot)


def reference(hidden, w_zx, w_bc, w_dt, conv_x, conv_x_bias, conv_bc, conv_bc_bias, a_log, dt_bias, d_skip, norm_gain, state_bank, conv_bank_x, conv_bank_bc, prompt_blocks, prompt_order, resume_slot):
    per_group = HEADS // GROUPS
    stream = hidden.reshape(N_SEQ, BLOCKS_DEV, BLOCK, WIDTH).transpose(1, 0, 2, 3).reshape(NBLOCKS, BLOCK, WIDTH)
    lengths = prompt_blocks[prompt_order].astype(jnp.int32)
    ends = jnp.cumsum(lengths).astype(jnp.int32)
    starts = (ends - lengths).astype(jnp.int32)
    slots = resume_slot[prompt_order].astype(jnp.int32)
    block_ids = jnp.arange(NBLOCKS, dtype=jnp.int32)
    owner = lax.optimization_barrier(jnp.sum((block_ids[:, None] >= ends[None, :]).astype(jnp.int32), axis=1)).astype(jnp.int32)
    first = jnp.any(block_ids[:, None] == starts[None, :], axis=1)
    block_slot = slots[owner]
    flat_zx = w_zx.reshape(WIDTH, 2 * INNER)
    flat_bc = w_bc.reshape(WIDTH, 2 * GROUP_STATE)
    kernel = jnp.concatenate([conv_x, conv_bc.reshape(KERNEL, 2 * GROUP_STATE)], axis=1).astype(jnp.float32)
    bias = jnp.concatenate([conv_x_bias, conv_bc_bias.reshape(2 * GROUP_STATE)], axis=0).astype(jnp.float32)
    bank_tails = jnp.concatenate([conv_bank_x, conv_bank_bc.reshape(BANK, KERNEL - 1, 2 * GROUP_STATE)], axis=2)
    rates = -jnp.exp(a_log)
    lower = jnp.arange(BLOCK)[:, None] >= jnp.arange(BLOCK)[None, :]
    head_group = jnp.arange(HEADS) // per_group

    def one_block(carry, inputs):
        state_prev, tail_prev = carry
        rows, is_first, slot = inputs
        zx = jnp.dot(rows, flat_zx, preferred_element_type=jnp.float32).astype(jnp.bfloat16)
        bc = jnp.dot(rows, flat_bc, preferred_element_type=jnp.float32).astype(jnp.bfloat16)
        dt_raw = jnp.dot(rows, w_dt, preferred_element_type=jnp.float32)
        gate = zx[:, :INNER]
        mixin = jnp.concatenate([zx[:, INNER:], bc], axis=1)
        pick = (slot == jnp.arange(BANK, dtype=jnp.int32)).astype(jnp.float32)
        bank_tail = jnp.einsum('r,rkz->kz', pick, bank_tails.astype(jnp.float32)).astype(jnp.bfloat16)
        init = jnp.einsum('r,rhpn->hpn', pick, state_bank, precision=lax.Precision.HIGHEST)
        tail = jnp.where(is_first, bank_tail, tail_prev)
        state_in = jnp.where(is_first, init, state_prev)
        padded = jnp.concatenate([tail, mixin], axis=0).astype(jnp.float32)
        acc = bias[None, :] + padded[0:BLOCK] * kernel[0]
        for k in range(1, KERNEL):
            acc = acc + padded[k:k + BLOCK] * kernel[k]
        conv = jax.nn.silu(acc).astype(jnp.bfloat16)
        xs = conv[:, :INNER].reshape(BLOCK, HEADS, HEAD_DIM)
        bs = conv[:, INNER:INNER + GROUP_STATE].reshape(BLOCK, GROUPS, STATE)
        cq = conv[:, INNER + GROUP_STATE:].reshape(BLOCK, GROUPS, STATE)
        dt = jax.nn.softplus(dt_raw + dt_bias[None, :])
        cum = jnp.cumsum(dt * rates[None, :], axis=0)
        scores = jnp.einsum('qgn,kgn->gqk', cq.astype(jnp.float32), bs.astype(jnp.float32))
        cum_h = cum.T
        diff = cum_h[:, :, None] - cum_h[:, None, :]
        damp = jnp.exp(jnp.where(lower[None], diff, -jnp.inf))
        mix = (scores[head_group] * damp * dt.T[:, None, :]).astype(jnp.bfloat16)
        y_intra = jnp.einsum('hqk,khp->qhp', mix.astype(jnp.float32), xs.astype(jnp.float32))
        last = cum[-1]
        read = jnp.einsum('qgn,gjpn->qgjp', cq.astype(jnp.float32), state_in.reshape(GROUPS, per_group, HEAD_DIM, STATE), precision=lax.Precision.HIGHEST).reshape(BLOCK, HEADS, HEAD_DIM)
        y = y_intra + jnp.exp(cum)[:, :, None] * read + d_skip[None, :, None] * xs.astype(jnp.float32)
        weighted = (xs.astype(jnp.float32) * (dt * jnp.exp(last[None, :] - cum))[:, :, None]).astype(jnp.bfloat16)
        local_state = jnp.einsum('qgjp,qgn->gjpn', weighted.reshape(BLOCK, GROUPS, per_group, HEAD_DIM).astype(jnp.float32), bs.astype(jnp.float32)).reshape(HEADS, HEAD_DIM, STATE)
        state_end = jnp.exp(last)[:, None, None] * state_in + local_state
        gated = y.reshape(BLOCK, INNER) * jax.nn.silu(gate.astype(jnp.float32))
        grouped = gated.reshape(BLOCK, GROUPS, INNER // GROUPS)
        scale = lax.rsqrt(lax.optimization_barrier(jnp.mean(grouped * grouped, axis=2, keepdims=True)) + 1e-05)
        out = (grouped * scale).reshape(BLOCK, INNER) * norm_gain[None, :]
        return ((state_end, mixin[BLOCK - (KERNEL - 1):]), out.astype(jnp.bfloat16))
    start = (jnp.zeros((HEADS, HEAD_DIM, STATE), jnp.float32), jnp.zeros((KERNEL - 1, INNER + 2 * GROUP_STATE), jnp.bfloat16))
    _, outs = lax.scan(one_block, start, (stream, first, block_slot))
    return outs.reshape(BLOCKS_DEV, N_SEQ, BLOCK, INNER).transpose(1, 0, 2, 3).reshape(TOKENS, INNER)
```

```python
import jax
import jax.numpy as jnp
from jax import lax
from jax.sharding import PartitionSpec as P

WIDTH = 4096
HEAD_DIM = 64
STATE = 128
BLOCK = 256
KERNEL = 4
BANK = 2


def from_behind(value, axis, steps):
    count = lax.axis_size(axis)
    pairs = [(source, (source + steps) % count) for source in range(count)]
    return lax.ppermute(value, axis, pairs)


def combine(earlier, later):
    return (earlier[0] * later[0], later[0][..., None, None] * earlier[1] + later[1])


def per_device(
    hidden,
    w_zx,
    w_bc,
    w_dt,
    conv_x,
    conv_x_bias,
    conv_bc,
    conv_bc_bias,
    a_log,
    dt_bias,
    d_skip,
    norm_gain,
    state_bank,
    conv_bank_x,
    conv_bank_bc,
    prompt_blocks,
    prompt_order,
    resume_slot,
):
    devices = lax.axis_size("seq")
    place = lax.axis_index("seq")
    rows_dev = hidden.shape[0]
    blocks = rows_dev // BLOCK
    inner_dev = w_zx.shape[2]
    gstate_dev = w_bc.shape[2]
    heads_dev = w_dt.shape[1]
    groups_dev = gstate_dev // STATE
    per_group = heads_dev // groups_dev
    channels = inner_dev + 2 * gstate_dev
    prompts = prompt_blocks.shape[0]
    flat_zx = w_zx.reshape(WIDTH, 2 * inner_dev)
    flat_bc = w_bc.reshape(WIDTH, 2 * gstate_dev)
    piece = lax.all_gather(hidden, "mp", axis=1, tiled=True)
    zx_sum = jnp.dot(piece, flat_zx, preferred_element_type=jnp.float32)
    bc_sum = jnp.dot(piece, flat_bc, preferred_element_type=jnp.float32)
    dt_raw = jnp.dot(piece, w_dt, preferred_element_type=jnp.float32)
    zx = zx_sum.astype(jnp.bfloat16)
    bc = bc_sum.astype(jnp.bfloat16)
    gate = zx[:, :inner_dev]
    mixin = jnp.concatenate([zx[:, inner_dev:], bc], axis=1).reshape(blocks, BLOCK, channels)
    own_tails = mixin[:, BLOCK - (KERNEL - 1) :, :]
    arrived = from_behind(own_tails, "seq", 1)
    wrapped = jnp.concatenate([jnp.zeros_like(arrived[:1]), arrived[:-1]], axis=0)
    before = jnp.where(place > 0, arrived, wrapped)
    prompt_ids = jnp.arange(prompts, dtype=jnp.int32)
    order_hot = (prompt_order[:, None] == prompt_ids[None, :]).astype(jnp.int32)
    lengths = jnp.sum(order_hot * prompt_blocks[None, :], axis=1)
    slots = jnp.sum(order_hot * resume_slot[None, :], axis=1)
    ends = jnp.cumsum(lengths)
    starts = ends - lengths
    stream_ids = jnp.arange(blocks, dtype=jnp.int32) * devices + place
    inside = (
        (stream_ids[:, None] >= starts[None, :]) & (stream_ids[:, None] < ends[None, :])
    ).astype(jnp.int32)
    block_slot = jnp.sum(inside * slots[None, :], axis=1)
    first = jnp.any(stream_ids[:, None] == starts[None, :], axis=1)
    pick = (block_slot[:, None] == jnp.arange(BANK, dtype=jnp.int32)[None, :]).astype(jnp.float32)
    bank_state = jnp.einsum("cr,rhpn->chpn", pick, state_bank, precision=lax.Precision.HIGHEST)
    bank_rows = jnp.concatenate(
        [conv_bank_x, conv_bank_bc.reshape(BANK, KERNEL - 1, 2 * gstate_dev)], axis=2
    )
    bank_tail = jnp.einsum("cr,rkz->ckz", pick, bank_rows.astype(jnp.float32)).astype(jnp.bfloat16)
    tail = jnp.where(first[:, None, None], bank_tail, before)
    kernel = jnp.concatenate([conv_x, conv_bc.reshape(KERNEL, 2 * gstate_dev)], axis=1)
    bias = jnp.concatenate([conv_x_bias, conv_bc_bias.reshape(2 * gstate_dev)], axis=0)
    padded = jnp.concatenate([tail, mixin], axis=1).astype(jnp.float32)
    acc = bias[None, None, :] + padded[:, 0:BLOCK] * kernel[0]
    for k in range(1, KERNEL):
        acc = acc + padded[:, k : k + BLOCK] * kernel[k]
    conv = jax.nn.silu(acc).astype(jnp.bfloat16)
    xs = conv[..., :inner_dev].reshape(blocks, BLOCK, groups_dev, per_group, HEAD_DIM)
    bs = conv[..., inner_dev : inner_dev + gstate_dev].reshape(blocks, BLOCK, groups_dev, STATE)
    cq = conv[..., inner_dev + gstate_dev :].reshape(blocks, BLOCK, groups_dev, STATE)
    dt = jax.nn.softplus(dt_raw.reshape(blocks, BLOCK, heads_dev) + dt_bias[None, None, :])
    cum = jnp.cumsum(dt * (-jnp.exp(a_log))[None, None, :], axis=1)
    scores = jnp.einsum("cqgn,ckgn->cgqk", cq, bs, preferred_element_type=jnp.float32)
    cum_h = cum.transpose(0, 2, 1)
    lower = jnp.arange(BLOCK)[:, None] >= jnp.arange(BLOCK)[None, :]
    damp = jnp.exp(
        jnp.where(lower[None, None], cum_h[:, :, :, None] - cum_h[:, :, None, :], -jnp.inf)
    )
    damp = damp.reshape(blocks, groups_dev, per_group, BLOCK, BLOCK)
    dt_h = dt.transpose(0, 2, 1).reshape(blocks, groups_dev, per_group, 1, BLOCK)
    mix = (scores[:, :, None] * damp * dt_h).astype(jnp.bfloat16)
    y_intra = jnp.einsum("cgjqk,ckgjp->cqgjp", mix, xs, preferred_element_type=jnp.float32)
    last = cum[:, -1, :]
    grow = jnp.exp(last)
    factor = (dt * jnp.exp(last[:, None, :] - cum)).reshape(blocks, BLOCK, groups_dev, per_group, 1)
    weighted = (xs.astype(jnp.float32) * factor).astype(jnp.bfloat16)
    local_state = jnp.einsum(
        "cqgjp,cqgn->cgjpn", weighted, bs, preferred_element_type=jnp.float32
    ).reshape(blocks, heads_dev, HEAD_DIM, STATE)
    step_a = jnp.where(first[:, None], 0.0, grow)
    step_b = local_state + jnp.where(
        first[:, None, None, None], grow[:, :, None, None] * bank_state, 0.0
    )
    run_a, run_b = step_a, step_b
    shift = 1
    while shift < devices:
        got_a, got_b = from_behind((run_a, run_b), "seq", shift)
        late = place >= shift
        lead_a = jnp.stack([jnp.where(late, got_a[0], 1.0), jnp.where(late, got_a[1], got_a[0])])
        lead_b = jnp.stack([jnp.where(late, got_b[0], 0.0), jnp.where(late, got_b[1], got_b[0])])
        run_a, run_b = combine((lead_a, lead_b), (run_a, run_b))
        shift *= 2
    top_a, top_b = combine((run_a[0], run_b[0]), (run_a[1], run_b[1]))
    run_b = jnp.stack([run_b[0], top_b])
    got_b = from_behind(run_b, "seq", 1)
    previous = jnp.stack([got_b[0], jnp.where(place >= 1, got_b[1], got_b[0])])
    state_in = jnp.where(first[:, None, None, None], bank_state, previous)
    read = jnp.einsum(
        "cqgn,cgjpn->cqgjp",
        cq.astype(jnp.float32),
        state_in.reshape(blocks, groups_dev, per_group, HEAD_DIM, STATE),
        precision=lax.Precision.HIGHEST,
    )
    growth = jnp.exp(cum).reshape(blocks, BLOCK, groups_dev, per_group, 1)
    skip = d_skip.reshape(1, 1, groups_dev, per_group, 1)
    y_total = y_intra + growth * read + skip * xs.astype(jnp.float32)
    gated = y_total.reshape(rows_dev, inner_dev) * jax.nn.silu(gate.astype(jnp.float32))
    grouped = gated.reshape(rows_dev, groups_dev, inner_dev // groups_dev)
    scale = lax.rsqrt(jnp.mean(grouped * grouped, axis=2, keepdims=True) + 1e-05)
    result = (grouped * scale).reshape(rows_dev, inner_dev) * norm_gain[None, :]
    return result.astype(jnp.bfloat16)


def solution(mesh):
    placed = (
        P("seq", "mp"),
        P(None, None, "mp"),
        P(None, None, "mp"),
        P(None, "mp"),
        P(None, "mp"),
        P("mp"),
        P(None, None, "mp"),
        P(None, "mp"),
        P("mp"),
        P("mp"),
        P("mp"),
        P("mp"),
        P(None, "mp", None, None),
        P(None, None, "mp"),
        P(None, None, None, "mp"),
        P(),
        P(),
        P(),
    )
    return jax.shard_map(
        per_device, mesh=mesh, in_specs=placed, out_specs=P("seq", "mp"), check_vma=False
    )
```

```python
import jax
import jax.numpy as jnp
from jax import lax
from jax.sharding import PartitionSpec as P

WIDTH = 4096
HEAD_DIM = 64
STATE = 128
BLOCK = 256
KERNEL = 4
BANK = 2


def from_behind(value, axis, steps):
    count = lax.axis_size(axis)
    pairs = [(source, (source + steps) % count) for source in range(count)]
    return lax.ppermute(value, axis, pairs)


def combine(earlier, later):
    return (earlier[0] * later[0], later[0][..., None, None] * earlier[1] + later[1])


def per_device(
    hidden,
    w_zx,
    w_bc,
    w_dt,
    conv_x,
    conv_x_bias,
    conv_bc,
    conv_bc_bias,
    a_log,
    dt_bias,
    d_skip,
    norm_gain,
    state_bank,
    conv_bank_x,
    conv_bank_bc,
    prompt_blocks,
    prompt_order,
    resume_slot,
):
    devices = lax.axis_size("seq")
    place = lax.axis_index("seq")
    rows_dev = hidden.shape[0]
    blocks = rows_dev // BLOCK
    inner_dev = w_zx.shape[2]
    gstate_dev = w_bc.shape[2]
    heads_dev = w_dt.shape[1]
    groups_dev = gstate_dev // STATE
    per_group = heads_dev // groups_dev
    channels = inner_dev + 2 * gstate_dev
    prompts = prompt_blocks.shape[0]
    flat_zx = w_zx.reshape(WIDTH, 2 * inner_dev)
    flat_bc = w_bc.reshape(WIDTH, 2 * gstate_dev)
    piece = lax.all_gather(hidden, "mp", axis=1, tiled=True)
    zx_sum = jnp.dot(piece, flat_zx, preferred_element_type=jnp.float32)
    bc_sum = jnp.dot(piece, flat_bc, preferred_element_type=jnp.float32)
    dt_raw = jnp.dot(piece, w_dt, preferred_element_type=jnp.float32)
    zx = zx_sum.astype(jnp.bfloat16)
    bc = bc_sum.astype(jnp.bfloat16)
    gate = zx[:, :inner_dev]
    mixin = jnp.concatenate([zx[:, inner_dev:], bc], axis=1).reshape(blocks, BLOCK, channels)
    own_tails = mixin[:, BLOCK - (KERNEL - 1) :, :]
    arrived = from_behind(own_tails, "seq", 1)
    wrapped = jnp.concatenate([jnp.zeros_like(arrived[:1]), arrived[:-1]], axis=0)
    before = jnp.where(place > 0, arrived, wrapped)
    prompt_ids = jnp.arange(prompts, dtype=jnp.int32)
    order_hot = (prompt_order[:, None] == prompt_ids[None, :]).astype(jnp.int32)
    lengths = jnp.sum(order_hot * prompt_blocks[None, :], axis=1)
    slots = jnp.sum(order_hot * resume_slot[None, :], axis=1)
    ends = jnp.cumsum(lengths)
    starts = ends - lengths
    stream_ids = jnp.arange(blocks, dtype=jnp.int32) * devices + place
    inside = (
        (stream_ids[:, None] >= starts[None, :]) & (stream_ids[:, None] < ends[None, :])
    ).astype(jnp.int32)
    block_slot = jnp.sum(inside * slots[None, :], axis=1)
    first = jnp.any(stream_ids[:, None] == starts[None, :], axis=1)
    pick = (block_slot[:, None] == jnp.arange(BANK, dtype=jnp.int32)[None, :]).astype(jnp.float32)
    bank_state = jnp.einsum("cr,rhpn->chpn", pick, state_bank, precision=lax.Precision.HIGHEST)
    bank_rows = jnp.concatenate(
        [conv_bank_x, conv_bank_bc.reshape(BANK, KERNEL - 1, 2 * gstate_dev)], axis=2
    )
    bank_tail = jnp.einsum("cr,rkz->ckz", pick, bank_rows.astype(jnp.float32)).astype(jnp.bfloat16)
    tail = jnp.where(first[:, None, None], bank_tail, before)
    kernel = jnp.concatenate([conv_x, conv_bc.reshape(KERNEL, 2 * gstate_dev)], axis=1)
    bias = jnp.concatenate([conv_x_bias, conv_bc_bias.reshape(2 * gstate_dev)], axis=0)
    padded = jnp.concatenate([tail, mixin], axis=1).astype(jnp.float32)
    acc = bias[None, None, :] + padded[:, 0:BLOCK] * kernel[0]
    for k in range(1, KERNEL):
        acc = acc + padded[:, k : k + BLOCK] * kernel[k]
    conv = jax.nn.silu(acc).astype(jnp.bfloat16)
    xs = conv[..., :inner_dev].reshape(blocks, BLOCK, groups_dev, per_group, HEAD_DIM)
    bs = conv[..., inner_dev : inner_dev + gstate_dev].reshape(blocks, BLOCK, groups_dev, STATE)
    cq = conv[..., inner_dev + gstate_dev :].reshape(blocks, BLOCK, groups_dev, STATE)
    dt = jax.nn.softplus(dt_raw.reshape(blocks, BLOCK, heads_dev) + dt_bias[None, None, :])
    cum = jnp.cumsum(dt * (-jnp.exp(a_log))[None, None, :], axis=1)
    scores = jnp.einsum("cqgn,ckgn->cgqk", cq, bs, preferred_element_type=jnp.float32)
    cum_h = cum.transpose(0, 2, 1)
    lower = jnp.arange(BLOCK)[:, None] >= jnp.arange(BLOCK)[None, :]
    damp = jnp.exp(
        jnp.where(lower[None, None], cum_h[:, :, :, None] - cum_h[:, :, None, :], -jnp.inf)
    )
    damp = damp.reshape(blocks, groups_dev, per_group, BLOCK, BLOCK)
    dt_h = dt.transpose(0, 2, 1).reshape(blocks, groups_dev, per_group, 1, BLOCK)
    mix = (scores[:, :, None] * damp * dt_h).astype(jnp.bfloat16)
    y_intra = jnp.einsum("cgjqk,ckgjp->cqgjp", mix, xs, preferred_element_type=jnp.float32)
    last = cum[:, -1, :]
    grow = jnp.exp(last)
    factor = (dt * jnp.exp(last[:, None, :] - cum)).reshape(blocks, BLOCK, groups_dev, per_group, 1)
    weighted = (xs.astype(jnp.float32) * factor).astype(jnp.bfloat16)
    local_state = jnp.einsum(
        "cqgjp,cqgn->cgjpn", weighted, bs, preferred_element_type=jnp.float32
    ).reshape(blocks, heads_dev, HEAD_DIM, STATE)
    step_a = jnp.where(first[:, None], 0.0, grow)
    step_b = local_state + jnp.where(
        first[:, None, None, None], grow[:, :, None, None] * bank_state, 0.0
    )
    core = place % 2
    chip = place // 2
    chips = devices // 2
    half = heads_dev // 2
    keep = lambda part, at: lax.dynamic_slice_in_dim(part, at * half, half, axis=1)
    pair = [(source, source ^ 1) for source in range(devices)]
    mine = (keep(step_a, core), keep(step_b, core))
    got = lax.ppermute((keep(step_a, 1 - core), keep(step_b, 1 - core)), "seq", pair)
    early = jax.tree.map(lambda own, other: jnp.where(core == 0, own, other), mine, got)
    later = jax.tree.map(lambda own, other: jnp.where(core == 0, other, own), mine, got)
    run_a, run_b = combine(early, later)
    span = 1
    while span < chips:
        got_a, got_b = from_behind((run_a, run_b), "seq", 2 * span)
        late = chip >= span
        lead_a = jnp.stack([jnp.where(late, got_a[0], 1.0), jnp.where(late, got_a[1], got_a[0])])
        lead_b = jnp.stack([jnp.where(late, got_b[0], 0.0), jnp.where(late, got_b[1], got_b[0])])
        run_a, run_b = combine((lead_a, lead_b), (run_a, run_b))
        span *= 2
    top_a, top_b = combine((run_a[0], run_b[0]), (run_a[1], run_b[1]))
    run_b = jnp.stack([run_b[0], top_b])
    got_b = from_behind(run_b, "seq", 2)
    before_chip = jnp.stack(
        [jnp.where(chip >= 1, got_b[0], 0.0), jnp.where(chip >= 1, got_b[1], got_b[0])]
    )
    after_early = early[0][..., None, None] * before_chip + early[1]
    own_part = jnp.where(core == 0, before_chip, after_early)
    other_part = lax.ppermute(jnp.where(core == 0, after_early, before_chip), "seq", pair)
    previous = jnp.where(
        core == 0,
        jnp.concatenate([own_part, other_part], axis=1),
        jnp.concatenate([other_part, own_part], axis=1),
    )
    state_in = jnp.where(first[:, None, None, None], bank_state, previous)
    read = jnp.einsum(
        "cqgn,cgjpn->cqgjp",
        cq.astype(jnp.float32),
        state_in.reshape(blocks, groups_dev, per_group, HEAD_DIM, STATE),
        precision=lax.Precision.HIGHEST,
    )
    growth = jnp.exp(cum).reshape(blocks, BLOCK, groups_dev, per_group, 1)
    skip = d_skip.reshape(1, 1, groups_dev, per_group, 1)
    y_total = y_intra + growth * read + skip * xs.astype(jnp.float32)
    gated = y_total.reshape(rows_dev, inner_dev) * jax.nn.silu(gate.astype(jnp.float32))
    grouped = gated.reshape(rows_dev, groups_dev, inner_dev // groups_dev)
    scale = lax.rsqrt(jnp.mean(grouped * grouped, axis=2, keepdims=True) + 1e-05)
    result = (grouped * scale).reshape(rows_dev, inner_dev) * norm_gain[None, :]
    return result.astype(jnp.bfloat16)


def solution(mesh):
    placed = (
        P("seq", "mp"),
        P(None, None, "mp"),
        P(None, None, "mp"),
        P(None, "mp"),
        P(None, "mp"),
        P("mp"),
        P(None, None, "mp"),
        P(None, "mp"),
        P("mp"),
        P("mp"),
        P("mp"),
        P("mp"),
        P(None, "mp", None, None),
        P(None, None, "mp"),
        P(None, None, None, "mp"),
        P(),
        P(),
        P(),
    )
    return jax.shard_map(
        per_device, mesh=mesh, in_specs=placed, out_specs=P("seq", "mp"), check_vma=False
    )
```

```python
import jax
import jax.numpy as jnp
from jax import lax
from jax.sharding import PartitionSpec as P

WIDTH = 4096
HEAD_DIM = 64
STATE = 128
BLOCK = 256
KERNEL = 4
BANK = 2
PIECES = 4


def from_behind(value, axis, steps):
    count = lax.axis_size(axis)
    pairs = [(source, (source + steps) % count) for source in range(count)]
    return lax.ppermute(value, axis, pairs)


def from_behind_split(value, axis, steps, pieces):
    parts = jnp.split(value, pieces, axis=1)
    return jnp.concatenate([from_behind(part, axis, steps) for part in parts], axis=1)


def combine(earlier, later):
    return (earlier[0] * later[0], later[0][..., None, None] * earlier[1] + later[1])


def per_device(
    hidden,
    w_zx,
    w_bc,
    w_dt,
    conv_x,
    conv_x_bias,
    conv_bc,
    conv_bc_bias,
    a_log,
    dt_bias,
    d_skip,
    norm_gain,
    state_bank,
    conv_bank_x,
    conv_bank_bc,
    prompt_blocks,
    prompt_order,
    resume_slot,
):
    devices = lax.axis_size("seq")
    place = lax.axis_index("seq")
    rows_dev = hidden.shape[0]
    blocks = rows_dev // BLOCK
    inner_dev = w_zx.shape[2]
    gstate_dev = w_bc.shape[2]
    heads_dev = w_dt.shape[1]
    groups_dev = gstate_dev // STATE
    per_group = heads_dev // groups_dev
    channels = inner_dev + 2 * gstate_dev
    prompts = prompt_blocks.shape[0]
    flat_zx = w_zx.reshape(WIDTH, 2 * inner_dev)
    flat_bc = w_bc.reshape(WIDTH, 2 * gstate_dev)
    piece = lax.all_gather(hidden, "mp", axis=1, tiled=True)
    zx_sum = jnp.dot(piece, flat_zx, preferred_element_type=jnp.float32)
    bc_sum = jnp.dot(piece, flat_bc, preferred_element_type=jnp.float32)
    dt_raw = jnp.dot(piece, w_dt, preferred_element_type=jnp.float32)
    zx = zx_sum.astype(jnp.bfloat16)
    bc = bc_sum.astype(jnp.bfloat16)
    gate = zx[:, :inner_dev]
    mixin = jnp.concatenate([zx[:, inner_dev:], bc], axis=1).reshape(blocks, BLOCK, channels)
    own_tails = mixin[:, BLOCK - (KERNEL - 1) :, :]
    arrived = from_behind(own_tails, "seq", 1)
    wrapped = jnp.concatenate([jnp.zeros_like(arrived[:1]), arrived[:-1]], axis=0)
    before = jnp.where(place > 0, arrived, wrapped)
    prompt_ids = jnp.arange(prompts, dtype=jnp.int32)
    order_hot = (prompt_order[:, None] == prompt_ids[None, :]).astype(jnp.int32)
    lengths = jnp.sum(order_hot * prompt_blocks[None, :], axis=1)
    slots = jnp.sum(order_hot * resume_slot[None, :], axis=1)
    ends = jnp.cumsum(lengths)
    starts = ends - lengths
    stream_ids = jnp.arange(blocks, dtype=jnp.int32) * devices + place
    inside = (
        (stream_ids[:, None] >= starts[None, :]) & (stream_ids[:, None] < ends[None, :])
    ).astype(jnp.int32)
    block_slot = jnp.sum(inside * slots[None, :], axis=1)
    first = jnp.any(stream_ids[:, None] == starts[None, :], axis=1)
    pick = (block_slot[:, None] == jnp.arange(BANK, dtype=jnp.int32)[None, :]).astype(jnp.float32)
    bank_state = jnp.einsum("cr,rhpn->chpn", pick, state_bank, precision=lax.Precision.HIGHEST)
    bank_rows = jnp.concatenate(
        [conv_bank_x, conv_bank_bc.reshape(BANK, KERNEL - 1, 2 * gstate_dev)], axis=2
    )
    bank_tail = jnp.einsum("cr,rkz->ckz", pick, bank_rows.astype(jnp.float32)).astype(jnp.bfloat16)
    tail = jnp.where(first[:, None, None], bank_tail, before)
    kernel = jnp.concatenate([conv_x, conv_bc.reshape(KERNEL, 2 * gstate_dev)], axis=1)
    bias = jnp.concatenate([conv_x_bias, conv_bc_bias.reshape(2 * gstate_dev)], axis=0)
    padded = jnp.concatenate([tail, mixin], axis=1).astype(jnp.float32)
    acc = bias[None, None, :] + padded[:, 0:BLOCK] * kernel[0]
    for k in range(1, KERNEL):
        acc = acc + padded[:, k : k + BLOCK] * kernel[k]
    conv = jax.nn.silu(acc).astype(jnp.bfloat16)
    xs = conv[..., :inner_dev].reshape(blocks, BLOCK, groups_dev, per_group, HEAD_DIM)
    bs = conv[..., inner_dev : inner_dev + gstate_dev].reshape(blocks, BLOCK, groups_dev, STATE)
    cq = conv[..., inner_dev + gstate_dev :].reshape(blocks, BLOCK, groups_dev, STATE)
    dt = jax.nn.softplus(dt_raw.reshape(blocks, BLOCK, heads_dev) + dt_bias[None, None, :])
    cum = jnp.cumsum(dt * (-jnp.exp(a_log))[None, None, :], axis=1)
    scores = jnp.einsum("cqgn,ckgn->cgqk", cq, bs, preferred_element_type=jnp.float32)
    cum_h = cum.transpose(0, 2, 1)
    lower = jnp.arange(BLOCK)[:, None] >= jnp.arange(BLOCK)[None, :]
    damp = jnp.exp(
        jnp.where(lower[None, None], cum_h[:, :, :, None] - cum_h[:, :, None, :], -jnp.inf)
    )
    damp = damp.reshape(blocks, groups_dev, per_group, BLOCK, BLOCK)
    dt_h = dt.transpose(0, 2, 1).reshape(blocks, groups_dev, per_group, 1, BLOCK)
    mix = (scores[:, :, None] * damp * dt_h).astype(jnp.bfloat16)
    y_intra = jnp.einsum("cgjqk,ckgjp->cqgjp", mix, xs, preferred_element_type=jnp.float32)
    last = cum[:, -1, :]
    grow = jnp.exp(last)
    factor = (dt * jnp.exp(last[:, None, :] - cum)).reshape(blocks, BLOCK, groups_dev, per_group, 1)
    weighted = (xs.astype(jnp.float32) * factor).astype(jnp.bfloat16)
    local_state = jnp.einsum(
        "cqgjp,cqgn->cgjpn", weighted, bs, preferred_element_type=jnp.float32
    ).reshape(blocks, heads_dev, HEAD_DIM, STATE)
    step_a = jnp.where(first[:, None], 0.0, grow)
    step_b = local_state + jnp.where(
        first[:, None, None, None], grow[:, :, None, None] * bank_state, 0.0
    )
    core = place % 2
    chip = place // 2
    chips = devices // 2
    half = heads_dev // 2
    keep = lambda part, at: lax.dynamic_slice_in_dim(part, at * half, half, axis=1)
    pair = [(source, source ^ 1) for source in range(devices)]
    mine = (keep(step_a, core), keep(step_b, core))
    got = lax.ppermute((keep(step_a, 1 - core), keep(step_b, 1 - core)), "seq", pair)
    early = jax.tree.map(lambda own, other: jnp.where(core == 0, own, other), mine, got)
    later = jax.tree.map(lambda own, other: jnp.where(core == 0, other, own), mine, got)
    run_a, run_b = combine(early, later)
    span = 1
    while span < chips:
        got_a = from_behind(run_a, "seq", 2 * span)
        got_b = from_behind_split(run_b, "seq", 2 * span, PIECES)
        late = chip >= span
        lead_a = jnp.stack([jnp.where(late, got_a[0], 1.0), jnp.where(late, got_a[1], got_a[0])])
        lead_b = jnp.stack([jnp.where(late, got_b[0], 0.0), jnp.where(late, got_b[1], got_b[0])])
        run_a, run_b = combine((lead_a, lead_b), (run_a, run_b))
        span *= 2
    top_a, top_b = combine((run_a[0], run_b[0]), (run_a[1], run_b[1]))
    run_b = jnp.stack([run_b[0], top_b])
    got_b = from_behind_split(run_b, "seq", 2, PIECES)
    before_chip = jnp.stack(
        [jnp.where(chip >= 1, got_b[0], 0.0), jnp.where(chip >= 1, got_b[1], got_b[0])]
    )
    after_early = early[0][..., None, None] * before_chip + early[1]
    own_part = jnp.where(core == 0, before_chip, after_early)
    other_part = lax.ppermute(jnp.where(core == 0, after_early, before_chip), "seq", pair)
    previous = jnp.where(
        core == 0,
        jnp.concatenate([own_part, other_part], axis=1),
        jnp.concatenate([other_part, own_part], axis=1),
    )
    state_in = jnp.where(first[:, None, None, None], bank_state, previous)
    read = jnp.einsum(
        "cqgn,cgjpn->cqgjp",
        cq.astype(jnp.float32),
        state_in.reshape(blocks, groups_dev, per_group, HEAD_DIM, STATE),
        precision=lax.Precision.HIGHEST,
    )
    growth = jnp.exp(cum).reshape(blocks, BLOCK, groups_dev, per_group, 1)
    skip = d_skip.reshape(1, 1, groups_dev, per_group, 1)
    y_total = y_intra + growth * read + skip * xs.astype(jnp.float32)
    gated = y_total.reshape(rows_dev, inner_dev) * jax.nn.silu(gate.astype(jnp.float32))
    grouped = gated.reshape(rows_dev, groups_dev, inner_dev // groups_dev)
    scale = lax.rsqrt(jnp.mean(grouped * grouped, axis=2, keepdims=True) + 1e-05)
    result = (grouped * scale).reshape(rows_dev, inner_dev) * norm_gain[None, :]
    return result.astype(jnp.bfloat16)


def solution(mesh):
    placed = (
        P("seq", "mp"),
        P(None, None, "mp"),
        P(None, None, "mp"),
        P(None, "mp"),
        P(None, "mp"),
        P("mp"),
        P(None, None, "mp"),
        P(None, "mp"),
        P("mp"),
        P("mp"),
        P("mp"),
        P("mp"),
        P(None, "mp", None, None),
        P(None, None, "mp"),
        P(None, None, None, "mp"),
        P(),
        P(),
        P(),
    )
    return jax.shard_map(
        per_device, mesh=mesh, in_specs=placed, out_specs=P("seq", "mp"), check_vma=False
    )
```

```python
import jax
import jax.numpy as jnp
from jax import lax
from jax.sharding import PartitionSpec as P

WIDTH = 4096
HEAD_DIM = 64
STATE = 128
BLOCK = 256
KERNEL = 4
BANK = 2


def from_behind(value, axis, steps):
    count = lax.axis_size(axis)
    pairs = [(source, (source + steps) % count) for source in range(count)]
    return lax.ppermute(value, axis, pairs)


def combine(earlier, later):
    return (earlier[0] * later[0], later[0][..., None, None] * earlier[1] + later[1])


def per_device(
    hidden,
    w_zx,
    w_bc,
    w_dt,
    conv_x,
    conv_x_bias,
    conv_bc,
    conv_bc_bias,
    a_log,
    dt_bias,
    d_skip,
    norm_gain,
    state_bank,
    conv_bank_x,
    conv_bank_bc,
    prompt_blocks,
    prompt_order,
    resume_slot,
):
    devices = lax.axis_size("seq")
    place = lax.axis_index("seq")
    rows_dev = hidden.shape[0]
    blocks = rows_dev // BLOCK
    inner_dev = w_zx.shape[2]
    gstate_dev = w_bc.shape[2]
    heads_dev = w_dt.shape[1]
    groups_dev = gstate_dev // STATE
    per_group = heads_dev // groups_dev
    channels = inner_dev + 2 * gstate_dev
    prompts = prompt_blocks.shape[0]
    flat_zx = w_zx.reshape(WIDTH, 2 * inner_dev)
    flat_bc = w_bc.reshape(WIDTH, 2 * gstate_dev)
    piece = lax.all_gather(hidden, "mp", axis=1, tiled=True)
    zx_sum = jnp.dot(piece, flat_zx, preferred_element_type=jnp.float32)
    bc_sum = jnp.dot(piece, flat_bc, preferred_element_type=jnp.float32)
    dt_raw = jnp.dot(piece, w_dt, preferred_element_type=jnp.float32)
    zx = zx_sum.astype(jnp.bfloat16)
    bc = bc_sum.astype(jnp.bfloat16)
    gate = zx[:, :inner_dev]
    mixin = jnp.concatenate([zx[:, inner_dev:], bc], axis=1).reshape(blocks, BLOCK, channels)
    own_tails = mixin[:, BLOCK - (KERNEL - 1) :, :]
    arrived = from_behind(own_tails, "seq", 1)
    wrapped = jnp.concatenate([jnp.zeros_like(arrived[:1]), arrived[:-1]], axis=0)
    before = jnp.where(place > 0, arrived, wrapped)
    prompt_ids = jnp.arange(prompts, dtype=jnp.int32)
    order_hot = (prompt_order[:, None] == prompt_ids[None, :]).astype(jnp.int32)
    lengths = jnp.sum(order_hot * prompt_blocks[None, :], axis=1)
    slots = jnp.sum(order_hot * resume_slot[None, :], axis=1)
    ends = jnp.cumsum(lengths)
    starts = ends - lengths
    stream_ids = jnp.arange(blocks, dtype=jnp.int32) * devices + place
    inside = (
        (stream_ids[:, None] >= starts[None, :]) & (stream_ids[:, None] < ends[None, :])
    ).astype(jnp.int32)
    block_slot = jnp.sum(inside * slots[None, :], axis=1)
    first = jnp.any(stream_ids[:, None] == starts[None, :], axis=1)
    pick = (block_slot[:, None] == jnp.arange(BANK, dtype=jnp.int32)[None, :]).astype(jnp.float32)
    bank_state = jnp.einsum("cr,rhpn->chpn", pick, state_bank, precision=lax.Precision.HIGHEST)
    bank_rows = jnp.concatenate(
        [conv_bank_x, conv_bank_bc.reshape(BANK, KERNEL - 1, 2 * gstate_dev)], axis=2
    )
    bank_tail = jnp.einsum("cr,rkz->ckz", pick, bank_rows.astype(jnp.float32)).astype(jnp.bfloat16)
    tail = jnp.where(first[:, None, None], bank_tail, before)
    kernel = jnp.concatenate([conv_x, conv_bc.reshape(KERNEL, 2 * gstate_dev)], axis=1)
    bias = jnp.concatenate([conv_x_bias, conv_bc_bias.reshape(2 * gstate_dev)], axis=0)
    padded = jnp.concatenate([tail, mixin], axis=1).astype(jnp.float32)
    acc = bias[None, None, :] + padded[:, 0:BLOCK] * kernel[0]
    for k in range(1, KERNEL):
        acc = acc + padded[:, k : k + BLOCK] * kernel[k]
    conv = jax.nn.silu(acc).astype(jnp.bfloat16)
    xs = conv[..., :inner_dev].reshape(blocks, BLOCK, groups_dev, per_group, HEAD_DIM)
    bs = conv[..., inner_dev : inner_dev + gstate_dev].reshape(blocks, BLOCK, groups_dev, STATE)
    cq = conv[..., inner_dev + gstate_dev :].reshape(blocks, BLOCK, groups_dev, STATE)
    dt = jax.nn.softplus(dt_raw.reshape(blocks, BLOCK, heads_dev) + dt_bias[None, None, :])
    cum = jnp.cumsum(dt * (-jnp.exp(a_log))[None, None, :], axis=1)
    scores = jnp.einsum("cqgn,ckgn->cgqk", cq, bs, preferred_element_type=jnp.float32)
    cum_h = cum.transpose(0, 2, 1)
    lower = jnp.arange(BLOCK)[:, None] >= jnp.arange(BLOCK)[None, :]
    damp = jnp.exp(
        jnp.where(lower[None, None], cum_h[:, :, :, None] - cum_h[:, :, None, :], -jnp.inf)
    )
    damp = damp.reshape(blocks, groups_dev, per_group, BLOCK, BLOCK)
    dt_h = dt.transpose(0, 2, 1).reshape(blocks, groups_dev, per_group, 1, BLOCK)
    mix = (scores[:, :, None] * damp * dt_h).astype(jnp.bfloat16)
    y_intra = jnp.einsum("cgjqk,ckgjp->cqgjp", mix, xs, preferred_element_type=jnp.float32)
    last = cum[:, -1, :]
    grow = jnp.exp(last)
    factor = (dt * jnp.exp(last[:, None, :] - cum)).reshape(blocks, BLOCK, groups_dev, per_group, 1)
    weighted = (xs.astype(jnp.float32) * factor).astype(jnp.bfloat16)
    local_state = jnp.einsum(
        "cqgjp,cqgn->cgjpn", weighted, bs, preferred_element_type=jnp.float32
    ).reshape(blocks, heads_dev, HEAD_DIM, STATE)
    step_a = jnp.where(first[:, None], 0.0, grow)
    step_b = local_state + jnp.where(
        first[:, None, None, None], grow[:, :, None, None] * bank_state, 0.0
    )
    core = place % 2
    chip = place // 2
    chips = devices // 2
    half = heads_dev // 2
    keep = lambda part, at: lax.dynamic_slice_in_dim(part, at * half, half, axis=1)
    pair = [(source, source ^ 1) for source in range(devices)]
    mine = (keep(step_a, core), keep(step_b, core))
    got = lax.ppermute((keep(step_a, 1 - core), keep(step_b, 1 - core)), "seq", pair)
    early = jax.tree.map(lambda own, other: jnp.where(core == 0, own, other), mine, got)
    later = jax.tree.map(lambda own, other: jnp.where(core == 0, other, own), mine, got)
    run_a, run_b = combine(early, later)
    prior_a, prior_b = jnp.ones_like(run_a), jnp.zeros_like(run_b)
    span = 1
    while span < chips:
        got_a, got_b = from_behind((run_a, run_b), "seq", 2 * span)
        late = chip >= span
        lead_a = jnp.stack([jnp.where(late, got_a[0], 1.0), jnp.where(late, got_a[1], got_a[0])])
        lead_b = jnp.stack([jnp.where(late, got_b[0], 0.0), jnp.where(late, got_b[1], got_b[0])])
        run_a, run_b = combine((lead_a, lead_b), (run_a, run_b))
        prior_a, prior_b = combine((lead_a, lead_b), (prior_a, prior_b))
        span *= 2
    lift_a, lift_b = combine((run_a[0], run_b[0]), (prior_a[1], prior_b[1]))
    before_chip = jnp.stack([prior_b[0], lift_b])
    after_early = early[0][..., None, None] * before_chip + early[1]
    own_part = jnp.where(core == 0, before_chip, after_early)
    other_part = lax.ppermute(jnp.where(core == 0, after_early, before_chip), "seq", pair)
    previous = jnp.where(
        core == 0,
        jnp.concatenate([own_part, other_part], axis=1),
        jnp.concatenate([other_part, own_part], axis=1),
    )
    state_in = jnp.where(first[:, None, None, None], bank_state, previous)
    read = jnp.einsum(
        "cqgn,cgjpn->cqgjp",
        cq.astype(jnp.float32),
        state_in.reshape(blocks, groups_dev, per_group, HEAD_DIM, STATE),
        precision=lax.Precision.HIGHEST,
    )
    growth = jnp.exp(cum).reshape(blocks, BLOCK, groups_dev, per_group, 1)
    skip = d_skip.reshape(1, 1, groups_dev, per_group, 1)
    y_total = y_intra + growth * read + skip * xs.astype(jnp.float32)
    gated = y_total.reshape(rows_dev, inner_dev) * jax.nn.silu(gate.astype(jnp.float32))
    grouped = gated.reshape(rows_dev, groups_dev, inner_dev // groups_dev)
    scale = lax.rsqrt(jnp.mean(grouped * grouped, axis=2, keepdims=True) + 1e-05)
    result = (grouped * scale).reshape(rows_dev, inner_dev) * norm_gain[None, :]
    return result.astype(jnp.bfloat16)


def solution(mesh):
    placed = (
        P("seq", "mp"),
        P(None, None, "mp"),
        P(None, None, "mp"),
        P(None, "mp"),
        P(None, "mp"),
        P("mp"),
        P(None, None, "mp"),
        P(None, "mp"),
        P("mp"),
        P("mp"),
        P("mp"),
        P("mp"),
        P(None, "mp", None, None),
        P(None, None, "mp"),
        P(None, None, None, "mp"),
        P(),
        P(),
        P(),
    )
    return jax.shard_map(
        per_device, mesh=mesh, in_specs=placed, out_specs=P("seq", "mp"), check_vma=False
    )
```

```python
import jax
import jax.numpy as jnp
from jax import lax
from jax.sharding import PartitionSpec as P

WIDTH = 4096
HEAD_DIM = 64
STATE = 128
BLOCK = 256
KERNEL = 4
BANK = 2


def from_behind(value, axis, steps):
    count = lax.axis_size(axis)
    pairs = [(source, (source + steps) % count) for source in range(count)]
    return lax.ppermute(value, axis, pairs)


def combine(earlier, later):
    return (earlier[0] * later[0], later[0][:, None, None] * earlier[1] + later[1])


def per_device(
    hidden,
    w_zx,
    w_bc,
    w_dt,
    conv_x,
    conv_x_bias,
    conv_bc,
    conv_bc_bias,
    a_log,
    dt_bias,
    d_skip,
    norm_gain,
    state_bank,
    conv_bank_x,
    conv_bank_bc,
    prompt_blocks,
    prompt_order,
    resume_slot,
):
    devices = lax.axis_size("seq")
    place = lax.axis_index("seq")
    rows_dev = hidden.shape[0]
    blocks = rows_dev // BLOCK
    inner_dev = w_zx.shape[2]
    gstate_dev = w_bc.shape[2]
    heads_dev = w_dt.shape[1]
    groups_dev = gstate_dev // STATE
    per_group = heads_dev // groups_dev
    channels = inner_dev + 2 * gstate_dev
    prompts = prompt_blocks.shape[0]
    flat_zx = w_zx.reshape(WIDTH, 2 * inner_dev)
    flat_bc = w_bc.reshape(WIDTH, 2 * gstate_dev)
    piece = lax.all_gather(hidden, "mp", axis=1, tiled=True)
    zx_sum = jnp.dot(piece, flat_zx, preferred_element_type=jnp.float32)
    bc_sum = jnp.dot(piece, flat_bc, preferred_element_type=jnp.float32)
    dt_raw = jnp.dot(piece, w_dt, preferred_element_type=jnp.float32)
    zx = zx_sum.astype(jnp.bfloat16)
    bc = bc_sum.astype(jnp.bfloat16)
    gate = zx[:, :inner_dev]
    mixin = jnp.concatenate([zx[:, inner_dev:], bc], axis=1).reshape(blocks, BLOCK, channels)
    own_tails = mixin[:, BLOCK - (KERNEL - 1) :, :]
    arrived = from_behind(own_tails, "seq", 1)
    wrapped = jnp.concatenate([jnp.zeros_like(arrived[:1]), arrived[:-1]], axis=0)
    before = jnp.where(place > 0, arrived, wrapped)
    prompt_ids = jnp.arange(prompts, dtype=jnp.int32)
    order_hot = (prompt_order[:, None] == prompt_ids[None, :]).astype(jnp.int32)
    lengths = jnp.sum(order_hot * prompt_blocks[None, :], axis=1)
    slots = jnp.sum(order_hot * resume_slot[None, :], axis=1)
    ends = jnp.cumsum(lengths)
    starts = ends - lengths
    stream_ids = jnp.arange(blocks, dtype=jnp.int32) * devices + place
    inside = (
        (stream_ids[:, None] >= starts[None, :]) & (stream_ids[:, None] < ends[None, :])
    ).astype(jnp.int32)
    block_slot = jnp.sum(inside * slots[None, :], axis=1)
    first = jnp.any(stream_ids[:, None] == starts[None, :], axis=1)
    pick = (block_slot[:, None] == jnp.arange(BANK, dtype=jnp.int32)[None, :]).astype(jnp.float32)
    bank_state = jnp.einsum("cr,rhpn->chpn", pick, state_bank, precision=lax.Precision.HIGHEST)
    bank_rows = jnp.concatenate(
        [conv_bank_x, conv_bank_bc.reshape(BANK, KERNEL - 1, 2 * gstate_dev)], axis=2
    )
    bank_tail = jnp.einsum("cr,rkz->ckz", pick, bank_rows.astype(jnp.float32)).astype(jnp.bfloat16)
    tail = jnp.where(first[:, None, None], bank_tail, before)
    kernel = jnp.concatenate([conv_x, conv_bc.reshape(KERNEL, 2 * gstate_dev)], axis=1)
    bias = jnp.concatenate([conv_x_bias, conv_bc_bias.reshape(2 * gstate_dev)], axis=0)
    padded = jnp.concatenate([tail, mixin], axis=1).astype(jnp.float32)
    acc = bias[None, None, :] + padded[:, 0:BLOCK] * kernel[0]
    for k in range(1, KERNEL):
        acc = acc + padded[:, k : k + BLOCK] * kernel[k]
    conv = jax.nn.silu(acc).astype(jnp.bfloat16)
    xs = conv[..., :inner_dev].reshape(blocks, BLOCK, groups_dev, per_group, HEAD_DIM)
    bs = conv[..., inner_dev : inner_dev + gstate_dev].reshape(blocks, BLOCK, groups_dev, STATE)
    cq = conv[..., inner_dev + gstate_dev :].reshape(blocks, BLOCK, groups_dev, STATE)
    dt = jax.nn.softplus(dt_raw.reshape(blocks, BLOCK, heads_dev) + dt_bias[None, None, :])
    cum = jnp.cumsum(dt * (-jnp.exp(a_log))[None, None, :], axis=1)
    scores = jnp.einsum("cqgn,ckgn->cgqk", cq, bs, preferred_element_type=jnp.float32)
    cum_h = cum.transpose(0, 2, 1)
    lower = jnp.arange(BLOCK)[:, None] >= jnp.arange(BLOCK)[None, :]
    damp = jnp.exp(
        jnp.where(lower[None, None], cum_h[:, :, :, None] - cum_h[:, :, None, :], -jnp.inf)
    )
    damp = damp.reshape(blocks, groups_dev, per_group, BLOCK, BLOCK)
    dt_h = dt.transpose(0, 2, 1).reshape(blocks, groups_dev, per_group, 1, BLOCK)
    mix = (scores[:, :, None] * damp * dt_h).astype(jnp.bfloat16)
    y_intra = jnp.einsum("cgjqk,ckgjp->cqgjp", mix, xs, preferred_element_type=jnp.float32)
    last = cum[:, -1, :]
    grow = jnp.exp(last)
    factor = (dt * jnp.exp(last[:, None, :] - cum)).reshape(blocks, BLOCK, groups_dev, per_group, 1)
    weighted = (xs.astype(jnp.float32) * factor).astype(jnp.bfloat16)
    local_state = jnp.einsum(
        "cqgjp,cqgn->cgjpn", weighted, bs, preferred_element_type=jnp.float32
    ).reshape(blocks, heads_dev, HEAD_DIM, STATE)
    step_a = jnp.where(first[:, None], 0.0, grow)
    step_b = local_state + jnp.where(
        first[:, None, None, None], grow[:, :, None, None] * bank_state, 0.0
    )
    core = place % 2
    chip = place // 2
    chips = devices // 2
    half = heads_dev // 2
    rows = blocks * half

    def keep(part, at):
        piece = lax.dynamic_slice_in_dim(part, at * half, half, axis=1)
        return piece.reshape((rows,) + part.shape[2:])

    pair = [(source, source ^ 1) for source in range(devices)]
    mine = (keep(step_a, core), keep(step_b, core))
    got = lax.ppermute((keep(step_a, 1 - core), keep(step_b, 1 - core)), "seq", pair)
    early = jax.tree.map(lambda own, other: jnp.where(core == 0, own, other), mine, got)
    later = jax.tree.map(lambda own, other: jnp.where(core == 0, other, own), mine, got)
    run_a, run_b = combine(early, later)
    prior_a, prior_b = jnp.ones_like(run_a), jnp.zeros_like(run_b)

    def wrap(part, neutral, late):
        moved = jnp.concatenate([jnp.full_like(part[:half], neutral), part[: rows - half]], axis=0)
        return jnp.where(late, part, moved)

    span = 1
    while span < chips:
        got_a, got_b = from_behind((run_a, run_b), "seq", 2 * span)
        late = chip >= span
        lead = (wrap(got_a, 1.0, late), wrap(got_b, 0.0, late))
        run_a, run_b = combine(lead, (run_a, run_b))
        prior_a, prior_b = combine(lead, (prior_a, prior_b))
        span *= 2
    lift = combine((run_a[:half], run_b[:half]), (prior_a[half:], prior_b[half:]))[1]
    before_chip = jnp.concatenate([prior_b[:half], lift], axis=0)
    after_early = early[0][:, None, None] * before_chip + early[1]
    own_part = jnp.where(core == 0, before_chip, after_early)
    other_part = lax.ppermute(jnp.where(core == 0, after_early, before_chip), "seq", pair)
    split_rows = lambda part: part.reshape((blocks, half) + part.shape[1:])
    own_part, other_part = split_rows(own_part), split_rows(other_part)
    previous = jnp.where(
        core == 0,
        jnp.concatenate([own_part, other_part], axis=1),
        jnp.concatenate([other_part, own_part], axis=1),
    )
    state_in = jnp.where(first[:, None, None, None], bank_state, previous)
    read = jnp.einsum(
        "cqgn,cgjpn->cqgjp",
        cq.astype(jnp.float32),
        state_in.reshape(blocks, groups_dev, per_group, HEAD_DIM, STATE),
        precision=lax.Precision.HIGHEST,
    )
    growth = jnp.exp(cum).reshape(blocks, BLOCK, groups_dev, per_group, 1)
    skip = d_skip.reshape(1, 1, groups_dev, per_group, 1)
    y_total = y_intra + growth * read + skip * xs.astype(jnp.float32)
    gated = y_total.reshape(rows_dev, inner_dev) * jax.nn.silu(gate.astype(jnp.float32))
    grouped = gated.reshape(rows_dev, groups_dev, inner_dev // groups_dev)
    scale = lax.rsqrt(jnp.mean(grouped * grouped, axis=2, keepdims=True) + 1e-05)
    result = (grouped * scale).reshape(rows_dev, inner_dev) * norm_gain[None, :]
    return result.astype(jnp.bfloat16)


def solution(mesh):
    placed = (
        P("seq", "mp"),
        P(None, None, "mp"),
        P(None, None, "mp"),
        P(None, "mp"),
        P(None, "mp"),
        P("mp"),
        P(None, None, "mp"),
        P(None, "mp"),
        P("mp"),
        P("mp"),
        P("mp"),
        P("mp"),
        P(None, "mp", None, None),
        P(None, None, "mp"),
        P(None, None, None, "mp"),
        P(),
        P(),
        P(),
    )
    return jax.shard_map(
        per_device, mesh=mesh, in_specs=placed, out_specs=P("seq", "mp"), check_vma=False
    )
```

```python
import jax
import jax.numpy as jnp
from jax import lax
from jax.sharding import PartitionSpec as P

WIDTH = 4096
HEAD_DIM = 64
STATE = 128
BLOCK = 256
KERNEL = 4
BANK = 2


def from_behind(value, axis, steps):
    count = lax.axis_size(axis)
    pairs = [(source, (source + steps) % count) for source in range(count)]
    return lax.ppermute(value, axis, pairs)


def combine(earlier, later):
    return (earlier[0] * later[0], later[0][:, None, None] * earlier[1] + later[1])


def per_device(
    hidden,
    w_zx,
    w_bc,
    w_dt,
    conv_x,
    conv_x_bias,
    conv_bc,
    conv_bc_bias,
    a_log,
    dt_bias,
    d_skip,
    norm_gain,
    state_bank,
    conv_bank_x,
    conv_bank_bc,
    prompt_blocks,
    prompt_order,
    resume_slot,
):
    devices = lax.axis_size("seq")
    place = lax.axis_index("seq")
    rows_dev = hidden.shape[0]
    blocks = rows_dev // BLOCK
    inner_dev = w_zx.shape[2]
    gstate_dev = w_bc.shape[2]
    heads_dev = w_dt.shape[1]
    groups_dev = gstate_dev // STATE
    per_group = heads_dev // groups_dev
    channels = inner_dev + 2 * gstate_dev
    prompts = prompt_blocks.shape[0]
    flat_zx = w_zx.reshape(WIDTH, 2 * inner_dev)
    flat_bc = w_bc.reshape(WIDTH, 2 * gstate_dev)
    piece = lax.all_gather(hidden, "mp", axis=1, tiled=True)
    zx_sum = jnp.dot(piece, flat_zx, preferred_element_type=jnp.float32)
    bc_sum = jnp.dot(piece, flat_bc, preferred_element_type=jnp.float32)
    dt_raw = jnp.dot(piece, w_dt, preferred_element_type=jnp.float32)
    zx = zx_sum.astype(jnp.bfloat16)
    bc = bc_sum.astype(jnp.bfloat16)
    gate = zx[:, :inner_dev]
    mixin = jnp.concatenate([zx[:, inner_dev:], bc], axis=1).reshape(blocks, BLOCK, channels)
    tail_rows = piece.reshape(blocks, BLOCK, WIDTH)[:, BLOCK - (KERNEL - 1) :, :]
    own_tails = jnp.concatenate(
        [
            jnp.einsum("ckw,wz->ckz", tail_rows, w_zx[:, 1, :], preferred_element_type=jnp.float32),
            jnp.einsum("ckw,wz->ckz", tail_rows, flat_bc, preferred_element_type=jnp.float32),
        ],
        axis=2,
    ).astype(jnp.bfloat16)
    arrived = from_behind(own_tails, "seq", 1)
    wrapped = jnp.concatenate([jnp.zeros_like(arrived[:1]), arrived[:-1]], axis=0)
    before = jnp.where(place > 0, arrived, wrapped)
    prompt_ids = jnp.arange(prompts, dtype=jnp.int32)
    order_hot = (prompt_order[:, None] == prompt_ids[None, :]).astype(jnp.int32)
    lengths = jnp.sum(order_hot * prompt_blocks[None, :], axis=1)
    slots = jnp.sum(order_hot * resume_slot[None, :], axis=1)
    ends = jnp.cumsum(lengths)
    starts = ends - lengths
    stream_ids = jnp.arange(blocks, dtype=jnp.int32) * devices + place
    inside = (
        (stream_ids[:, None] >= starts[None, :]) & (stream_ids[:, None] < ends[None, :])
    ).astype(jnp.int32)
    block_slot = jnp.sum(inside * slots[None, :], axis=1)
    first = jnp.any(stream_ids[:, None] == starts[None, :], axis=1)
    pick = (block_slot[:, None] == jnp.arange(BANK, dtype=jnp.int32)[None, :]).astype(jnp.float32)
    bank_state = jnp.einsum("cr,rhpn->chpn", pick, state_bank, precision=lax.Precision.HIGHEST)
    bank_rows = jnp.concatenate(
        [conv_bank_x, conv_bank_bc.reshape(BANK, KERNEL - 1, 2 * gstate_dev)], axis=2
    )
    bank_tail = jnp.einsum("cr,rkz->ckz", pick, bank_rows.astype(jnp.float32)).astype(jnp.bfloat16)
    tail = jnp.where(first[:, None, None], bank_tail, before)
    kernel = jnp.concatenate([conv_x, conv_bc.reshape(KERNEL, 2 * gstate_dev)], axis=1)
    bias = jnp.concatenate([conv_x_bias, conv_bc_bias.reshape(2 * gstate_dev)], axis=0)
    padded = jnp.concatenate([tail, mixin], axis=1).astype(jnp.float32)
    acc = bias[None, None, :] + padded[:, 0:BLOCK] * kernel[0]
    for k in range(1, KERNEL):
        acc = acc + padded[:, k : k + BLOCK] * kernel[k]
    conv = jax.nn.silu(acc).astype(jnp.bfloat16)
    xs = conv[..., :inner_dev].reshape(blocks, BLOCK, groups_dev, per_group, HEAD_DIM)
    bs = conv[..., inner_dev : inner_dev + gstate_dev].reshape(blocks, BLOCK, groups_dev, STATE)
    cq = conv[..., inner_dev + gstate_dev :].reshape(blocks, BLOCK, groups_dev, STATE)
    dt = jax.nn.softplus(dt_raw.reshape(blocks, BLOCK, heads_dev) + dt_bias[None, None, :])
    cum = jnp.cumsum(dt * (-jnp.exp(a_log))[None, None, :], axis=1)
    scores = jnp.einsum("cqgn,ckgn->cgqk", cq, bs, preferred_element_type=jnp.float32)
    cum_h = cum.transpose(0, 2, 1)
    lower = jnp.arange(BLOCK)[:, None] >= jnp.arange(BLOCK)[None, :]
    damp = jnp.exp(
        jnp.where(lower[None, None], cum_h[:, :, :, None] - cum_h[:, :, None, :], -jnp.inf)
    )
    damp = damp.reshape(blocks, groups_dev, per_group, BLOCK, BLOCK)
    dt_h = dt.transpose(0, 2, 1).reshape(blocks, groups_dev, per_group, 1, BLOCK)
    mix = (scores[:, :, None] * damp * dt_h).astype(jnp.bfloat16)
    y_intra = jnp.einsum("cgjqk,ckgjp->cqgjp", mix, xs, preferred_element_type=jnp.float32)
    last = cum[:, -1, :]
    grow = jnp.exp(last)
    factor = (dt * jnp.exp(last[:, None, :] - cum)).reshape(blocks, BLOCK, groups_dev, per_group, 1)
    weighted = (xs.astype(jnp.float32) * factor).astype(jnp.bfloat16)
    local_state = jnp.einsum(
        "cqgjp,cqgn->cgjpn", weighted, bs, preferred_element_type=jnp.float32
    ).reshape(blocks, heads_dev, HEAD_DIM, STATE)
    step_a = jnp.where(first[:, None], 0.0, grow)
    step_b = local_state + jnp.where(
        first[:, None, None, None], grow[:, :, None, None] * bank_state, 0.0
    )
    core = place % 2
    chip = place // 2
    chips = devices // 2
    half = heads_dev // 2
    rows = blocks * half

    def keep(part, at):
        chosen = jnp.where(at == 0, part[:, :half], part[:, half:])
        return chosen.reshape((rows,) + part.shape[2:])

    pair = [(source, source ^ 1) for source in range(devices)]
    mine = (keep(step_a, core), keep(step_b, core))
    got = lax.ppermute((keep(step_a, 1 - core), keep(step_b, 1 - core)), "seq", pair)
    early = jax.tree.map(lambda own, other: jnp.where(core == 0, own, other), mine, got)
    later = jax.tree.map(lambda own, other: jnp.where(core == 0, other, own), mine, got)
    run_a, run_b = combine(early, later)
    prior_a, prior_b = jnp.ones_like(run_a), jnp.zeros_like(run_b)

    def wrap(part, neutral, late):
        moved = jnp.concatenate([jnp.full_like(part[:half], neutral), part[: rows - half]], axis=0)
        return jnp.where(late, part, moved)

    span = 1
    while span < chips:
        got_a, got_b = from_behind((run_a, run_b), "seq", 2 * span)
        late = chip >= span
        lead = (wrap(got_a, 1.0, late), wrap(got_b, 0.0, late))
        run_a, run_b = combine(lead, (run_a, run_b))
        prior_a, prior_b = combine(lead, (prior_a, prior_b))
        span *= 2
    lift = combine((run_a[:half], run_b[:half]), (prior_a[half:], prior_b[half:]))[1]
    before_chip = jnp.concatenate([prior_b[:half], lift], axis=0)
    after_early = early[0][:, None, None] * before_chip + early[1]
    own_part = jnp.where(core == 0, before_chip, after_early)
    other_part = lax.ppermute(jnp.where(core == 0, after_early, before_chip), "seq", pair)
    split_rows = lambda part: part.reshape((blocks, half) + part.shape[1:])
    own_part, other_part = split_rows(own_part), split_rows(other_part)
    previous = jnp.where(
        core == 0,
        jnp.concatenate([own_part, other_part], axis=1),
        jnp.concatenate([other_part, own_part], axis=1),
    )
    state_in = jnp.where(first[:, None, None, None], bank_state, previous)
    read = jnp.einsum(
        "cqgn,cgmn->cqgm",
        cq.astype(jnp.float32),
        state_in.reshape(blocks, groups_dev, per_group * HEAD_DIM, STATE),
        precision=lax.Precision.HIGHEST,
    ).reshape(blocks, BLOCK, groups_dev, per_group, HEAD_DIM)
    growth = jnp.exp(cum).reshape(blocks, BLOCK, groups_dev, per_group, 1)
    skip = d_skip.reshape(1, 1, groups_dev, per_group, 1)
    y_total = y_intra + growth * read + skip * xs.astype(jnp.float32)
    gated = y_total.reshape(rows_dev, inner_dev) * jax.nn.silu(gate.astype(jnp.float32))
    grouped = gated.reshape(rows_dev, groups_dev, inner_dev // groups_dev)
    scale = lax.rsqrt(jnp.mean(grouped * grouped, axis=2, keepdims=True) + 1e-05)
    result = (grouped * scale).reshape(rows_dev, inner_dev) * norm_gain[None, :]
    return result.astype(jnp.bfloat16)


def solution(mesh):
    placed = (
        P("seq", "mp"),
        P(None, None, "mp"),
        P(None, None, "mp"),
        P(None, "mp"),
        P(None, "mp"),
        P("mp"),
        P(None, None, "mp"),
        P(None, "mp"),
        P("mp"),
        P("mp"),
        P("mp"),
        P("mp"),
        P(None, "mp", None, None),
        P(None, None, "mp"),
        P(None, None, None, "mp"),
        P(),
        P(),
        P(),
    )
    return jax.shard_map(
        per_device, mesh=mesh, in_specs=placed, out_specs=P("seq", "mp"), check_vma=False
    )
```

```python
import jax
import jax.numpy as jnp
from jax import lax
from jax.sharding import PartitionSpec as P

WIDTH = 4096
HEAD_DIM = 64
STATE = 128
BLOCK = 256
KERNEL = 4
BANK = 2


def from_behind(value, axis, steps):
    count = lax.axis_size(axis)
    pairs = [(source, (source + steps) % count) for source in range(count)]
    return lax.ppermute(value, axis, pairs)


def combine(earlier, later):
    return (earlier[0] * later[0], later[0][:, None, None] * earlier[1] + later[1])


def per_device(
    hidden,
    w_zx,
    w_bc,
    w_dt,
    conv_x,
    conv_x_bias,
    conv_bc,
    conv_bc_bias,
    a_log,
    dt_bias,
    d_skip,
    norm_gain,
    state_bank,
    conv_bank_x,
    conv_bank_bc,
    prompt_blocks,
    prompt_order,
    resume_slot,
):
    devices = lax.axis_size("seq")
    place = lax.axis_index("seq")
    rows_dev = hidden.shape[0]
    blocks = rows_dev // BLOCK
    inner_dev = w_zx.shape[2]
    gstate_dev = w_bc.shape[2]
    heads_dev = w_dt.shape[1]
    groups_dev = gstate_dev // STATE
    per_group = heads_dev // groups_dev
    channels = inner_dev + 2 * gstate_dev
    prompts = prompt_blocks.shape[0]
    flat_zx = w_zx.reshape(WIDTH, 2 * inner_dev)
    flat_bc = w_bc.reshape(WIDTH, 2 * gstate_dev)
    piece = lax.all_gather(hidden, "mp", axis=1, tiled=True)
    zx_sum = jnp.dot(piece, flat_zx, preferred_element_type=jnp.float32)
    bc_sum = jnp.dot(piece, flat_bc, preferred_element_type=jnp.float32)
    dt_raw = jnp.dot(piece, w_dt, preferred_element_type=jnp.float32)
    zx = zx_sum.astype(jnp.bfloat16)
    bc = bc_sum.astype(jnp.bfloat16)
    gate = zx[:, :inner_dev]
    mixin = jnp.concatenate([zx[:, inner_dev:], bc], axis=1).reshape(blocks, BLOCK, channels)
    own_tails = mixin[:, BLOCK - (KERNEL - 1) :, :]
    arrived = from_behind(own_tails, "seq", 1)
    wrapped = jnp.concatenate([jnp.zeros_like(arrived[:1]), arrived[:-1]], axis=0)
    before = jnp.where(place > 0, arrived, wrapped)
    prompt_ids = jnp.arange(prompts, dtype=jnp.int32)
    order_hot = (prompt_order[:, None] == prompt_ids[None, :]).astype(jnp.int32)
    lengths = jnp.sum(order_hot * prompt_blocks[None, :], axis=1)
    slots = jnp.sum(order_hot * resume_slot[None, :], axis=1)
    ends = jnp.cumsum(lengths)
    starts = ends - lengths
    stream_ids = jnp.arange(blocks, dtype=jnp.int32) * devices + place
    inside = (
        (stream_ids[:, None] >= starts[None, :]) & (stream_ids[:, None] < ends[None, :])
    ).astype(jnp.int32)
    block_slot = jnp.sum(inside * slots[None, :], axis=1)
    first = jnp.any(stream_ids[:, None] == starts[None, :], axis=1)
    pick = (block_slot[:, None] == jnp.arange(BANK, dtype=jnp.int32)[None, :]).astype(jnp.float32)
    bank_state = jnp.einsum("cr,rhpn->chpn", pick, state_bank, precision=lax.Precision.HIGHEST)
    bank_rows = jnp.concatenate(
        [conv_bank_x, conv_bank_bc.reshape(BANK, KERNEL - 1, 2 * gstate_dev)], axis=2
    )
    bank_tail = jnp.einsum("cr,rkz->ckz", pick, bank_rows.astype(jnp.float32)).astype(jnp.bfloat16)
    tail = jnp.where(first[:, None, None], bank_tail, before)
    kernel = jnp.concatenate([conv_x, conv_bc.reshape(KERNEL, 2 * gstate_dev)], axis=1)
    bias = jnp.concatenate([conv_x_bias, conv_bc_bias.reshape(2 * gstate_dev)], axis=0)
    padded = jnp.concatenate([tail, mixin], axis=1).astype(jnp.float32)
    acc = bias[None, None, :] + padded[:, 0:BLOCK] * kernel[0]
    for k in range(1, KERNEL):
        acc = acc + padded[:, k : k + BLOCK] * kernel[k]
    conv = jax.nn.silu(acc).astype(jnp.bfloat16)
    xs = conv[..., :inner_dev].reshape(blocks, BLOCK, groups_dev, per_group, HEAD_DIM)
    bs = conv[..., inner_dev : inner_dev + gstate_dev].reshape(blocks, BLOCK, groups_dev, STATE)
    cq = conv[..., inner_dev + gstate_dev :].reshape(blocks, BLOCK, groups_dev, STATE)
    dt = jax.nn.softplus(dt_raw.reshape(blocks, BLOCK, heads_dev) + dt_bias[None, None, :])
    cum = jnp.cumsum(dt * (-jnp.exp(a_log))[None, None, :], axis=1)
    scores = jnp.einsum("cqgn,ckgn->cgqk", cq, bs, preferred_element_type=jnp.float32)
    cum_h = cum.transpose(0, 2, 1)
    lower = jnp.arange(BLOCK)[:, None] >= jnp.arange(BLOCK)[None, :]
    damp = jnp.exp(
        jnp.where(lower[None, None], cum_h[:, :, :, None] - cum_h[:, :, None, :], -jnp.inf)
    )
    damp = damp.reshape(blocks, groups_dev, per_group, BLOCK, BLOCK)
    dt_h = dt.transpose(0, 2, 1).reshape(blocks, groups_dev, per_group, 1, BLOCK)
    mix = (scores[:, :, None] * damp * dt_h).astype(jnp.bfloat16)
    y_intra = jnp.einsum("cgjqk,ckgjp->cqgjp", mix, xs, preferred_element_type=jnp.float32)
    last = cum[:, -1, :]
    grow = jnp.exp(last)
    factor = (dt * jnp.exp(last[:, None, :] - cum)).reshape(blocks, BLOCK, groups_dev, per_group, 1)
    weighted = (xs.astype(jnp.float32) * factor).astype(jnp.bfloat16)
    local_state = jnp.einsum(
        "cqgjp,cqgn->cgjpn", weighted, bs, preferred_element_type=jnp.float32
    ).reshape(blocks, heads_dev, HEAD_DIM, STATE)
    step_a = jnp.where(first[:, None], 0.0, grow)
    step_b = local_state + jnp.where(
        first[:, None, None, None], grow[:, :, None, None] * bank_state, 0.0
    )
    core = place % 2
    chip = place // 2
    chips = devices // 2
    half = heads_dev // 2
    rows = blocks * half

    def keep(part, at):
        piece = lax.dynamic_slice_in_dim(part, at * half, half, axis=1)
        return piece.reshape((rows,) + part.shape[2:])

    pair = [(source, source ^ 1) for source in range(devices)]
    mine = (keep(step_a, core), keep(step_b, core))
    got = lax.ppermute((keep(step_a, 1 - core), keep(step_b, 1 - core)), "seq", pair)
    early = jax.tree.map(lambda own, other: jnp.where(core == 0, own, other), mine, got)
    later = jax.tree.map(lambda own, other: jnp.where(core == 0, other, own), mine, got)
    run_b = combine(early, later)[1]
    gathered = lax.all_gather(step_a, "seq")
    grown = gathered[0::2] * gathered[1::2]
    grown = grown.transpose(1, 0, 2).reshape(2 * chips, heads_dev)
    grown = jnp.where(core == 0, grown[:, :half], grown[:, half:])
    ahead = lambda part, back: jnp.concatenate([jnp.ones_like(part[:back]), part[: part.shape[0] - back]], axis=0)

    def window(low, high):
        total = jnp.ones_like(grown)
        for back in range(low, high):
            total = total * ahead(grown, back)
        spots = jnp.stack([lax.dynamic_index_in_dim(total, chip, keepdims=False),
                           lax.dynamic_index_in_dim(total, chips + chip, keepdims=False)])
        return spots

    quarter = half // 2
    groups = lambda part: [part.reshape((blocks, 2, quarter) + part.shape[1:])[:, g].reshape((blocks * quarter,) + part.shape[1:]) for g in range(2)]
    weights = lambda spots: [spots[:, g * quarter:(g + 1) * quarter].reshape(blocks * quarter) for g in range(2)]
    lanes = groups(run_b)
    priors = [jnp.zeros_like(lane) for lane in lanes]
    spans = [1 << i for i in range(chips.bit_length() - 1)]
    turn = len(spans) // 2
    orders = [spans, spans[turn:] + spans[:turn]]

    def wrap(part, late):
        moved = jnp.concatenate([jnp.zeros_like(part[:quarter]), part[: part.shape[0] - quarter]], axis=0)
        return jnp.where(late, part, moved)

    for step in range(len(orders[0])):
        for g in range(2):
            span = orders[g][step]
            got = from_behind(lanes[g], "seq", 2 * span)
            lead = wrap(got, chip >= span)
            inner_w = weights(window(0, span))[g]
            outer_w = weights(window(1, span))[g]
            lanes[g] = inner_w[:, None, None] * lead + lanes[g]
            priors[g] = outer_w[:, None, None] * lead + priors[g]
    lift_w = weights(window(1, chips))
    joined = []
    for g in range(2):
        lift = lift_w[g][quarter:, None, None] * lanes[g][:quarter] + priors[g][quarter:]
        joined.append(jnp.concatenate([priors[g][:quarter], lift], axis=0))
    before_chip = jnp.concatenate(
        [part.reshape((blocks, quarter) + part.shape[1:]) for part in joined], axis=1
    ).reshape(run_b.shape)
    after_early = early[0][:, None, None] * before_chip + early[1]
    own_part = jnp.where(core == 0, before_chip, after_early)
    other_part = lax.ppermute(jnp.where(core == 0, after_early, before_chip), "seq", pair)
    split_rows = lambda part: part.reshape((blocks, half) + part.shape[1:])
    own_part, other_part = split_rows(own_part), split_rows(other_part)
    previous = jnp.where(
        core == 0,
        jnp.concatenate([own_part, other_part], axis=1),
        jnp.concatenate([other_part, own_part], axis=1),
    )
    state_in = jnp.where(first[:, None, None, None], bank_state, previous)
    read = jnp.einsum(
        "cqgn,cgjpn->cqgjp",
        cq.astype(jnp.float32),
        state_in.reshape(blocks, groups_dev, per_group, HEAD_DIM, STATE),
        precision=lax.Precision.HIGHEST,
    )
    growth = jnp.exp(cum).reshape(blocks, BLOCK, groups_dev, per_group, 1)
    skip = d_skip.reshape(1, 1, groups_dev, per_group, 1)
    y_total = y_intra + growth * read + skip * xs.astype(jnp.float32)
    gated = y_total.reshape(rows_dev, inner_dev) * jax.nn.silu(gate.astype(jnp.float32))
    grouped = gated.reshape(rows_dev, groups_dev, inner_dev // groups_dev)
    scale = lax.rsqrt(jnp.mean(grouped * grouped, axis=2, keepdims=True) + 1e-05)
    result = (grouped * scale).reshape(rows_dev, inner_dev) * norm_gain[None, :]
    return result.astype(jnp.bfloat16)


def solution(mesh):
    placed = (
        P("seq", "mp"),
        P(None, None, "mp"),
        P(None, None, "mp"),
        P(None, "mp"),
        P(None, "mp"),
        P("mp"),
        P(None, None, "mp"),
        P(None, "mp"),
        P("mp"),
        P("mp"),
        P("mp"),
        P("mp"),
        P(None, "mp", None, None),
        P(None, None, "mp"),
        P(None, None, None, "mp"),
        P(),
        P(),
        P(),
    )
    return jax.shard_map(
        per_device, mesh=mesh, in_specs=placed, out_specs=P("seq", "mp"), check_vma=False
    )
```

```python
import jax
import jax.numpy as jnp
from jax import lax
from jax.sharding import PartitionSpec as P

WIDTH = 4096
HEAD_DIM = 64
STATE = 128
BLOCK = 256
KERNEL = 4
BANK = 2


def from_behind(value, axis, steps):
    count = lax.axis_size(axis)
    pairs = [(source, (source + steps) % count) for source in range(count)]
    return lax.ppermute(value, axis, pairs)


def combine(earlier, later):
    return (earlier[0] * later[0], later[0][:, None, None] * earlier[1] + later[1])


def per_device(
    hidden,
    w_zx,
    w_bc,
    w_dt,
    conv_x,
    conv_x_bias,
    conv_bc,
    conv_bc_bias,
    a_log,
    dt_bias,
    d_skip,
    norm_gain,
    state_bank,
    conv_bank_x,
    conv_bank_bc,
    prompt_blocks,
    prompt_order,
    resume_slot,
):
    devices = lax.axis_size("seq")
    place = lax.axis_index("seq")
    rows_dev = hidden.shape[0]
    blocks = rows_dev // BLOCK
    inner_dev = w_zx.shape[2]
    gstate_dev = w_bc.shape[2]
    heads_dev = w_dt.shape[1]
    groups_dev = gstate_dev // STATE
    per_group = heads_dev // groups_dev
    channels = inner_dev + 2 * gstate_dev
    prompts = prompt_blocks.shape[0]
    flat_zx = w_zx.reshape(WIDTH, 2 * inner_dev)
    flat_bc = w_bc.reshape(WIDTH, 2 * gstate_dev)
    piece = lax.all_gather(hidden, "mp", axis=1, tiled=True)
    zx_sum = jnp.dot(piece, flat_zx, preferred_element_type=jnp.float32)
    bc_sum = jnp.dot(piece, flat_bc, preferred_element_type=jnp.float32)
    dt_raw = jnp.dot(piece, w_dt, preferred_element_type=jnp.float32)
    zx = zx_sum.astype(jnp.bfloat16)
    bc = bc_sum.astype(jnp.bfloat16)
    gate = zx[:, :inner_dev]
    mixin = jnp.concatenate([zx[:, inner_dev:], bc], axis=1).reshape(blocks, BLOCK, channels)
    own_tails = mixin[:, BLOCK - (KERNEL - 1) :, :]
    arrived = from_behind(own_tails, "seq", 1)
    wrapped = jnp.concatenate([jnp.zeros_like(arrived[:1]), arrived[:-1]], axis=0)
    before = jnp.where(place > 0, arrived, wrapped)
    prompt_ids = jnp.arange(prompts, dtype=jnp.int32)
    order_hot = (prompt_order[:, None] == prompt_ids[None, :]).astype(jnp.int32)
    lengths = jnp.sum(order_hot * prompt_blocks[None, :], axis=1)
    slots = jnp.sum(order_hot * resume_slot[None, :], axis=1)
    ends = jnp.cumsum(lengths)
    starts = ends - lengths
    stream_ids = jnp.arange(blocks, dtype=jnp.int32) * devices + place
    inside = (
        (stream_ids[:, None] >= starts[None, :]) & (stream_ids[:, None] < ends[None, :])
    ).astype(jnp.int32)
    block_slot = jnp.sum(inside * slots[None, :], axis=1)
    first = jnp.any(stream_ids[:, None] == starts[None, :], axis=1)
    pick = (block_slot[:, None] == jnp.arange(BANK, dtype=jnp.int32)[None, :]).astype(jnp.float32)
    bank_state = jnp.einsum("cr,rhpn->chpn", pick, state_bank, precision=lax.Precision.HIGHEST)
    bank_rows = jnp.concatenate(
        [conv_bank_x, conv_bank_bc.reshape(BANK, KERNEL - 1, 2 * gstate_dev)], axis=2
    )
    bank_tail = jnp.einsum("cr,rkz->ckz", pick, bank_rows.astype(jnp.float32)).astype(jnp.bfloat16)
    tail = jnp.where(first[:, None, None], bank_tail, before)
    kernel = jnp.concatenate([conv_x, conv_bc.reshape(KERNEL, 2 * gstate_dev)], axis=1)
    bias = jnp.concatenate([conv_x_bias, conv_bc_bias.reshape(2 * gstate_dev)], axis=0)
    padded = jnp.concatenate([tail, mixin], axis=1).astype(jnp.float32)
    acc = bias[None, None, :] + padded[:, 0:BLOCK] * kernel[0]
    for k in range(1, KERNEL):
        acc = acc + padded[:, k : k + BLOCK] * kernel[k]
    conv = jax.nn.silu(acc).astype(jnp.bfloat16)
    xs = conv[..., :inner_dev].reshape(blocks, BLOCK, groups_dev, per_group, HEAD_DIM)
    bs = conv[..., inner_dev : inner_dev + gstate_dev].reshape(blocks, BLOCK, groups_dev, STATE)
    cq = conv[..., inner_dev + gstate_dev :].reshape(blocks, BLOCK, groups_dev, STATE)
    dt = jax.nn.softplus(dt_raw.reshape(blocks, BLOCK, heads_dev) + dt_bias[None, None, :])
    cum = jnp.cumsum(dt * (-jnp.exp(a_log))[None, None, :], axis=1)
    scores = jnp.einsum("cqgn,ckgn->cgqk", cq, bs, preferred_element_type=jnp.float32)
    cum_h = cum.transpose(0, 2, 1)
    lower = jnp.arange(BLOCK)[:, None] >= jnp.arange(BLOCK)[None, :]
    damp = jnp.exp(
        jnp.where(lower[None, None], cum_h[:, :, :, None] - cum_h[:, :, None, :], -jnp.inf)
    )
    damp = damp.reshape(blocks, groups_dev, per_group, BLOCK, BLOCK)
    dt_h = dt.transpose(0, 2, 1).reshape(blocks, groups_dev, per_group, 1, BLOCK)
    mix = (scores[:, :, None] * damp * dt_h).astype(jnp.bfloat16)
    y_intra = jnp.einsum("cgjqk,ckgjp->cqgjp", mix, xs, preferred_element_type=jnp.float32)
    last = cum[:, -1, :]
    grow = jnp.exp(last)
    factor = (dt * jnp.exp(last[:, None, :] - cum)).reshape(blocks, BLOCK, groups_dev, per_group, 1)
    weighted = (xs.astype(jnp.float32) * factor).astype(jnp.bfloat16)
    local_state = jnp.einsum(
        "cqgjp,cqgn->cgjpn", weighted, bs, preferred_element_type=jnp.float32
    ).reshape(blocks, heads_dev, HEAD_DIM, STATE)
    step_a = jnp.where(first[:, None], 0.0, grow)
    step_b = local_state + jnp.where(
        first[:, None, None, None], grow[:, :, None, None] * bank_state, 0.0
    )
    core = place % 2
    chip = place // 2
    chips = devices // 2
    half = heads_dev // 2
    rows = blocks * half

    def keep(part, at):
        piece = lax.dynamic_slice_in_dim(part, at * half, half, axis=1)
        return piece.reshape((rows,) + part.shape[2:])

    pair = [(source, source ^ 1) for source in range(devices)]
    mine = (keep(step_a, core), keep(step_b, core))
    got = lax.ppermute((keep(step_a, 1 - core), keep(step_b, 1 - core)), "seq", pair)
    early = jax.tree.map(lambda own, other: jnp.where(core == 0, own, other), mine, got)
    later = jax.tree.map(lambda own, other: jnp.where(core == 0, other, own), mine, got)
    run_b = combine(early, later)[1]
    spans = [1 << i for i in range(chips.bit_length() - 1)]
    inner_at, outer_at = {}, {}
    ra = combine(early, later)[0]
    pa = jnp.ones_like(ra)
    for span in spans:
        inner_at[span], outer_at[span] = ra, pa
        got = from_behind(ra, "seq", 2 * span)
        moved = jnp.concatenate([jnp.ones_like(got[:half]), got[: rows - half]], axis=0)
        lead = jnp.where(chip >= span, got, moved)
        ra, pa = lead * ra, lead * pa
    outer_at[chips] = pa
    quarter = half // 2
    groups = lambda part: [part.reshape((blocks, 2, quarter) + part.shape[1:])[:, g].reshape((blocks * quarter,) + part.shape[1:]) for g in range(2)]
    weights = lambda flat: [flat.reshape(blocks, half)[:, g * quarter:(g + 1) * quarter].reshape(blocks * quarter) for g in range(2)]
    lanes = groups(run_b)
    priors = [jnp.zeros_like(lane) for lane in lanes]
    turn = len(spans) // 2
    orders = [spans, spans[turn:] + spans[:turn]]

    def wrap(part, late):
        moved = jnp.concatenate([jnp.zeros_like(part[:quarter]), part[: part.shape[0] - quarter]], axis=0)
        return jnp.where(late, part, moved)

    for step in range(len(orders[0])):
        for g in range(2):
            span = orders[g][step]
            got = from_behind(lanes[g], "seq", 2 * span)
            lead = wrap(got, chip >= span)
            inner_w = weights(inner_at[span])[g]
            outer_w = weights(outer_at[span])[g]
            lanes[g] = inner_w[:, None, None] * lead + lanes[g]
            priors[g] = outer_w[:, None, None] * lead + priors[g]
    lift_w = weights(outer_at[chips])
    joined = []
    for g in range(2):
        lift = lift_w[g][quarter:, None, None] * lanes[g][:quarter] + priors[g][quarter:]
        joined.append(jnp.concatenate([priors[g][:quarter], lift], axis=0))
    before_chip = jnp.concatenate(
        [part.reshape((blocks, quarter) + part.shape[1:]) for part in joined], axis=1
    ).reshape(run_b.shape)
    after_early = early[0][:, None, None] * before_chip + early[1]
    own_part = jnp.where(core == 0, before_chip, after_early)
    other_part = lax.ppermute(jnp.where(core == 0, after_early, before_chip), "seq", pair)
    split_rows = lambda part: part.reshape((blocks, half) + part.shape[1:])
    own_part, other_part = split_rows(own_part), split_rows(other_part)
    previous = jnp.where(
        core == 0,
        jnp.concatenate([own_part, other_part], axis=1),
        jnp.concatenate([other_part, own_part], axis=1),
    )
    state_in = jnp.where(first[:, None, None, None], bank_state, previous)
    read = jnp.einsum(
        "cqgn,cgjpn->cqgjp",
        cq.astype(jnp.float32),
        state_in.reshape(blocks, groups_dev, per_group, HEAD_DIM, STATE),
        precision=lax.Precision.HIGHEST,
    )
    growth = jnp.exp(cum).reshape(blocks, BLOCK, groups_dev, per_group, 1)
    skip = d_skip.reshape(1, 1, groups_dev, per_group, 1)
    y_total = y_intra + growth * read + skip * xs.astype(jnp.float32)
    gated = y_total.reshape(rows_dev, inner_dev) * jax.nn.silu(gate.astype(jnp.float32))
    grouped = gated.reshape(rows_dev, groups_dev, inner_dev // groups_dev)
    scale = lax.rsqrt(jnp.mean(grouped * grouped, axis=2, keepdims=True) + 1e-05)
    result = (grouped * scale).reshape(rows_dev, inner_dev) * norm_gain[None, :]
    return result.astype(jnp.bfloat16)


def solution(mesh):
    placed = (
        P("seq", "mp"),
        P(None, None, "mp"),
        P(None, None, "mp"),
        P(None, "mp"),
        P(None, "mp"),
        P("mp"),
        P(None, None, "mp"),
        P(None, "mp"),
        P("mp"),
        P("mp"),
        P("mp"),
        P("mp"),
        P(None, "mp", None, None),
        P(None, None, "mp"),
        P(None, None, None, "mp"),
        P(),
        P(),
        P(),
    )
    return jax.shard_map(
        per_device, mesh=mesh, in_specs=placed, out_specs=P("seq", "mp"), check_vma=False
    )
```

```python
import jax
import jax.numpy as jnp
from jax import lax
from jax.sharding import PartitionSpec as P

WIDTH = 4096
HEAD_DIM = 64
STATE = 128
BLOCK = 256
KERNEL = 4
BANK = 2


def from_behind(value, axis, steps):
    count = lax.axis_size(axis)
    pairs = [(source, (source + steps) % count) for source in range(count)]
    return lax.ppermute(value, axis, pairs)


def combine(earlier, later):
    return (earlier[0] * later[0], later[0][:, None, None] * earlier[1] + later[1])


def per_device(
    hidden,
    w_zx,
    w_bc,
    w_dt,
    conv_x,
    conv_x_bias,
    conv_bc,
    conv_bc_bias,
    a_log,
    dt_bias,
    d_skip,
    norm_gain,
    state_bank,
    conv_bank_x,
    conv_bank_bc,
    prompt_blocks,
    prompt_order,
    resume_slot,
):
    devices = lax.axis_size("seq")
    place = lax.axis_index("seq")
    rows_dev = hidden.shape[0]
    blocks = rows_dev // BLOCK
    inner_dev = w_zx.shape[2]
    gstate_dev = w_bc.shape[2]
    heads_dev = w_dt.shape[1]
    groups_dev = gstate_dev // STATE
    per_group = heads_dev // groups_dev
    channels = inner_dev + 2 * gstate_dev
    prompts = prompt_blocks.shape[0]
    flat_zx = w_zx.reshape(WIDTH, 2 * inner_dev)
    flat_bc = w_bc.reshape(WIDTH, 2 * gstate_dev)
    owners = lax.axis_size("mp")
    column = lax.axis_index("mp")
    split = hidden.shape[1] // 2
    front = lax.all_gather(hidden[:, :split], "mp", axis=1, tiled=True)
    back = jnp.zeros((rows_dev, owners, split), hidden.dtype)
    for steps in range(owners):
        moved = hidden[:, split:] if steps == 0 else from_behind(hidden[:, split:], "mp", steps)
        back = lax.dynamic_update_slice(back, moved[:, None, :], (0, (column - steps) % owners, 0))
    piece = jnp.concatenate(
        [front.reshape(rows_dev, owners, 1, split), back.reshape(rows_dev, owners, 1, split)], axis=2
    ).reshape(rows_dev, owners * 2 * split)
    zx_sum = jnp.dot(piece, flat_zx, preferred_element_type=jnp.float32)
    bc_sum = jnp.dot(piece, flat_bc, preferred_element_type=jnp.float32)
    dt_raw = jnp.dot(piece, w_dt, preferred_element_type=jnp.float32)
    zx = zx_sum.astype(jnp.bfloat16)
    bc = bc_sum.astype(jnp.bfloat16)
    gate = zx[:, :inner_dev]
    mixin = jnp.concatenate([zx[:, inner_dev:], bc], axis=1).reshape(blocks, BLOCK, channels)
    own_tails = mixin[:, BLOCK - (KERNEL - 1) :, :]
    arrived = from_behind(own_tails, "seq", 1)
    wrapped = jnp.concatenate([jnp.zeros_like(arrived[:1]), arrived[:-1]], axis=0)
    before = jnp.where(place > 0, arrived, wrapped)
    prompt_ids = jnp.arange(prompts, dtype=jnp.int32)
    order_hot = (prompt_order[:, None] == prompt_ids[None, :]).astype(jnp.int32)
    lengths = jnp.sum(order_hot * prompt_blocks[None, :], axis=1)
    slots = jnp.sum(order_hot * resume_slot[None, :], axis=1)
    ends = jnp.cumsum(lengths)
    starts = ends - lengths
    stream_ids = jnp.arange(blocks, dtype=jnp.int32) * devices + place
    inside = (
        (stream_ids[:, None] >= starts[None, :]) & (stream_ids[:, None] < ends[None, :])
    ).astype(jnp.int32)
    block_slot = jnp.sum(inside * slots[None, :], axis=1)
    first = jnp.any(stream_ids[:, None] == starts[None, :], axis=1)
    pick = (block_slot[:, None] == jnp.arange(BANK, dtype=jnp.int32)[None, :]).astype(jnp.float32)
    bank_state = jnp.einsum("cr,rhpn->chpn", pick, state_bank, precision=lax.Precision.HIGHEST)
    bank_rows = jnp.concatenate(
        [conv_bank_x, conv_bank_bc.reshape(BANK, KERNEL - 1, 2 * gstate_dev)], axis=2
    )
    bank_tail = jnp.einsum("cr,rkz->ckz", pick, bank_rows.astype(jnp.float32)).astype(jnp.bfloat16)
    tail = jnp.where(first[:, None, None], bank_tail, before)
    kernel = jnp.concatenate([conv_x, conv_bc.reshape(KERNEL, 2 * gstate_dev)], axis=1)
    bias = jnp.concatenate([conv_x_bias, conv_bc_bias.reshape(2 * gstate_dev)], axis=0)
    padded = jnp.concatenate([tail, mixin], axis=1).astype(jnp.float32)
    acc = bias[None, None, :] + padded[:, 0:BLOCK] * kernel[0]
    for k in range(1, KERNEL):
        acc = acc + padded[:, k : k + BLOCK] * kernel[k]
    conv = jax.nn.silu(acc).astype(jnp.bfloat16)
    xs = conv[..., :inner_dev].reshape(blocks, BLOCK, groups_dev, per_group, HEAD_DIM)
    bs = conv[..., inner_dev : inner_dev + gstate_dev].reshape(blocks, BLOCK, groups_dev, STATE)
    cq = conv[..., inner_dev + gstate_dev :].reshape(blocks, BLOCK, groups_dev, STATE)
    dt = jax.nn.softplus(dt_raw.reshape(blocks, BLOCK, heads_dev) + dt_bias[None, None, :])
    cum = jnp.cumsum(dt * (-jnp.exp(a_log))[None, None, :], axis=1)
    scores = jnp.einsum("cqgn,ckgn->cgqk", cq, bs, preferred_element_type=jnp.float32)
    cum_h = cum.transpose(0, 2, 1)
    lower = jnp.arange(BLOCK)[:, None] >= jnp.arange(BLOCK)[None, :]
    damp = jnp.exp(
        jnp.where(lower[None, None], cum_h[:, :, :, None] - cum_h[:, :, None, :], -jnp.inf)
    )
    damp = damp.reshape(blocks, groups_dev, per_group, BLOCK, BLOCK)
    dt_h = dt.transpose(0, 2, 1).reshape(blocks, groups_dev, per_group, 1, BLOCK)
    mix = (scores[:, :, None] * damp * dt_h).astype(jnp.bfloat16)
    y_intra = jnp.einsum("cgjqk,ckgjp->cqgjp", mix, xs, preferred_element_type=jnp.float32)
    last = cum[:, -1, :]
    grow = jnp.exp(last)
    factor = (dt * jnp.exp(last[:, None, :] - cum)).reshape(blocks, BLOCK, groups_dev, per_group, 1)
    weighted = (xs.astype(jnp.float32) * factor).astype(jnp.bfloat16)
    local_state = jnp.einsum(
        "cqgjp,cqgn->cgjpn", weighted, bs, preferred_element_type=jnp.float32
    ).reshape(blocks, heads_dev, HEAD_DIM, STATE)
    step_a = jnp.where(first[:, None], 0.0, grow)
    step_b = local_state + jnp.where(
        first[:, None, None, None], grow[:, :, None, None] * bank_state, 0.0
    )
    core = place % 2
    chip = place // 2
    chips = devices // 2
    half = heads_dev // 2
    rows = blocks * half

    def keep(part, at):
        piece = lax.dynamic_slice_in_dim(part, at * half, half, axis=1)
        return piece.reshape((rows,) + part.shape[2:])

    pair = [(source, source ^ 1) for source in range(devices)]
    mine = (keep(step_a, core), keep(step_b, core))
    got = lax.ppermute((keep(step_a, 1 - core), keep(step_b, 1 - core)), "seq", pair)
    early = jax.tree.map(lambda own, other: jnp.where(core == 0, own, other), mine, got)
    later = jax.tree.map(lambda own, other: jnp.where(core == 0, other, own), mine, got)
    run_a, run_b = combine(early, later)
    prior_a, prior_b = jnp.ones_like(run_a), jnp.zeros_like(run_b)

    def wrap(part, neutral, late):
        moved = jnp.concatenate([jnp.full_like(part[:half], neutral), part[: rows - half]], axis=0)
        return jnp.where(late, part, moved)

    span = 1
    while span < chips:
        got_a, got_b = from_behind((run_a, run_b), "seq", 2 * span)
        late = chip >= span
        lead = (wrap(got_a, 1.0, late), wrap(got_b, 0.0, late))
        run_a, run_b = combine(lead, (run_a, run_b))
        prior_a, prior_b = combine(lead, (prior_a, prior_b))
        span *= 2
    lift = combine((run_a[:half], run_b[:half]), (prior_a[half:], prior_b[half:]))[1]
    before_chip = jnp.concatenate([prior_b[:half], lift], axis=0)
    after_early = early[0][:, None, None] * before_chip + early[1]
    own_part = jnp.where(core == 0, before_chip, after_early)
    other_part = lax.ppermute(jnp.where(core == 0, after_early, before_chip), "seq", pair)
    split_rows = lambda part: part.reshape((blocks, half) + part.shape[1:])
    own_part, other_part = split_rows(own_part), split_rows(other_part)
    previous = jnp.where(
        core == 0,
        jnp.concatenate([own_part, other_part], axis=1),
        jnp.concatenate([other_part, own_part], axis=1),
    )
    state_in = jnp.where(first[:, None, None, None], bank_state, previous)
    read = jnp.einsum(
        "cqgn,cgjpn->cqgjp",
        cq.astype(jnp.float32),
        state_in.reshape(blocks, groups_dev, per_group, HEAD_DIM, STATE),
        precision=lax.Precision.HIGHEST,
    )
    growth = jnp.exp(cum).reshape(blocks, BLOCK, groups_dev, per_group, 1)
    skip = d_skip.reshape(1, 1, groups_dev, per_group, 1)
    y_total = y_intra + growth * read + skip * xs.astype(jnp.float32)
    gated = y_total.reshape(rows_dev, inner_dev) * jax.nn.silu(gate.astype(jnp.float32))
    grouped = gated.reshape(rows_dev, groups_dev, inner_dev // groups_dev)
    scale = lax.rsqrt(jnp.mean(grouped * grouped, axis=2, keepdims=True) + 1e-05)
    result = (grouped * scale).reshape(rows_dev, inner_dev) * norm_gain[None, :]
    return result.astype(jnp.bfloat16)


def solution(mesh):
    placed = (
        P("seq", "mp"),
        P(None, None, "mp"),
        P(None, None, "mp"),
        P(None, "mp"),
        P(None, "mp"),
        P("mp"),
        P(None, None, "mp"),
        P(None, "mp"),
        P("mp"),
        P("mp"),
        P("mp"),
        P("mp"),
        P(None, "mp", None, None),
        P(None, None, "mp"),
        P(None, None, None, "mp"),
        P(),
        P(),
        P(),
    )
    return jax.shard_map(
        per_device, mesh=mesh, in_specs=placed, out_specs=P("seq", "mp"), check_vma=False
    )
```

```python
import jax
import jax.numpy as jnp
from jax import lax
from jax.sharding import PartitionSpec as P

WIDTH = 4096
HEAD_DIM = 64
STATE = 128
BLOCK = 256
KERNEL = 4
BANK = 2


def from_behind(value, axis, steps):
    count = lax.axis_size(axis)
    pairs = [(source, (source + steps) % count) for source in range(count)]
    return lax.ppermute(value, axis, pairs)


def combine(earlier, later):
    return (earlier[0] * later[0], later[0][:, None, None] * earlier[1] + later[1])


def per_device(
    hidden,
    w_zx,
    w_bc,
    w_dt,
    conv_x,
    conv_x_bias,
    conv_bc,
    conv_bc_bias,
    a_log,
    dt_bias,
    d_skip,
    norm_gain,
    state_bank,
    conv_bank_x,
    conv_bank_bc,
    prompt_blocks,
    prompt_order,
    resume_slot,
):
    devices = lax.axis_size("seq")
    place = lax.axis_index("seq")
    rows_dev = hidden.shape[0]
    blocks = rows_dev // BLOCK
    inner_dev = w_zx.shape[2]
    gstate_dev = w_bc.shape[2]
    heads_dev = w_dt.shape[1]
    groups_dev = gstate_dev // STATE
    per_group = heads_dev // groups_dev
    channels = inner_dev + 2 * gstate_dev
    prompts = prompt_blocks.shape[0]
    flat_zx = w_zx.reshape(WIDTH, 2 * inner_dev)
    flat_bc = w_bc.reshape(WIDTH, 2 * gstate_dev)
    piece = lax.all_gather(hidden, "mp", axis=1, tiled=True)
    zx_sum = jnp.dot(piece, flat_zx, preferred_element_type=jnp.float32)
    bc_sum = jnp.dot(piece, flat_bc, preferred_element_type=jnp.float32)
    dt_raw = jnp.dot(piece, w_dt, preferred_element_type=jnp.float32)
    zx = zx_sum.astype(jnp.bfloat16)
    bc = bc_sum.astype(jnp.bfloat16)
    gate = zx[:, :inner_dev]
    mixin = jnp.concatenate([zx[:, inner_dev:], bc], axis=1).reshape(blocks, BLOCK, channels)
    tail_rows = piece.reshape(blocks, BLOCK, WIDTH)[:, BLOCK - (KERNEL - 1) :, :]
    tail_zx = jnp.einsum("ckw,wz->ckz", tail_rows, flat_zx[:, inner_dev:], preferred_element_type=jnp.float32)
    tail_bc = jnp.einsum("ckw,wz->ckz", tail_rows, flat_bc, preferred_element_type=jnp.float32)
    own_tails = jnp.concatenate([tail_zx, tail_bc], axis=2).astype(jnp.bfloat16)
    arrived = from_behind(own_tails, "seq", 1)
    wrapped = jnp.concatenate([jnp.zeros_like(arrived[:1]), arrived[:-1]], axis=0)
    before = jnp.where(place > 0, arrived, wrapped)
    prompt_ids = jnp.arange(prompts, dtype=jnp.int32)
    order_hot = (prompt_order[:, None] == prompt_ids[None, :]).astype(jnp.int32)
    lengths = jnp.sum(order_hot * prompt_blocks[None, :], axis=1)
    slots = jnp.sum(order_hot * resume_slot[None, :], axis=1)
    ends = jnp.cumsum(lengths)
    starts = ends - lengths
    stream_ids = jnp.arange(blocks, dtype=jnp.int32) * devices + place
    inside = (
        (stream_ids[:, None] >= starts[None, :]) & (stream_ids[:, None] < ends[None, :])
    ).astype(jnp.int32)
    block_slot = jnp.sum(inside * slots[None, :], axis=1)
    first = jnp.any(stream_ids[:, None] == starts[None, :], axis=1)
    pick = (block_slot[:, None] == jnp.arange(BANK, dtype=jnp.int32)[None, :]).astype(jnp.float32)
    bank_state = jnp.einsum("cr,rhpn->chpn", pick, state_bank, precision=lax.Precision.HIGHEST)
    bank_rows = jnp.concatenate(
        [conv_bank_x, conv_bank_bc.reshape(BANK, KERNEL - 1, 2 * gstate_dev)], axis=2
    )
    bank_tail = jnp.einsum("cr,rkz->ckz", pick, bank_rows.astype(jnp.float32)).astype(jnp.bfloat16)
    tail = jnp.where(first[:, None, None], bank_tail, before)
    kernel = jnp.concatenate([conv_x, conv_bc.reshape(KERNEL, 2 * gstate_dev)], axis=1)
    bias = jnp.concatenate([conv_x_bias, conv_bc_bias.reshape(2 * gstate_dev)], axis=0)
    padded = jnp.concatenate([tail, mixin], axis=1).astype(jnp.float32)
    acc = bias[None, None, :] + padded[:, 0:BLOCK] * kernel[0]
    for k in range(1, KERNEL):
        acc = acc + padded[:, k : k + BLOCK] * kernel[k]
    conv = jax.nn.silu(acc).astype(jnp.bfloat16)
    xs = conv[..., :inner_dev].reshape(blocks, BLOCK, groups_dev, per_group, HEAD_DIM)
    bs = conv[..., inner_dev : inner_dev + gstate_dev].reshape(blocks, BLOCK, groups_dev, STATE)
    cq = conv[..., inner_dev + gstate_dev :].reshape(blocks, BLOCK, groups_dev, STATE)
    dt = jax.nn.softplus(dt_raw.reshape(blocks, BLOCK, heads_dev) + dt_bias[None, None, :])
    cum = jnp.cumsum(dt * (-jnp.exp(a_log))[None, None, :], axis=1)
    scores = jnp.einsum("cqgn,ckgn->cgqk", cq, bs, preferred_element_type=jnp.float32)
    cum_h = cum.transpose(0, 2, 1)
    lower = jnp.arange(BLOCK)[:, None] >= jnp.arange(BLOCK)[None, :]
    damp = jnp.exp(
        jnp.where(lower[None, None], cum_h[:, :, :, None] - cum_h[:, :, None, :], -jnp.inf)
    )
    damp = damp.reshape(blocks, groups_dev, per_group, BLOCK, BLOCK)
    dt_h = dt.transpose(0, 2, 1).reshape(blocks, groups_dev, per_group, 1, BLOCK)
    mix = (scores[:, :, None] * damp * dt_h).astype(jnp.bfloat16)
    y_intra = jnp.einsum("cgjqk,ckgjp->cqgjp", mix, xs, preferred_element_type=jnp.float32)
    last = cum[:, -1, :]
    grow = jnp.exp(last)
    factor = (dt * jnp.exp(last[:, None, :] - cum)).reshape(blocks, BLOCK, groups_dev, per_group, 1)
    weighted = (xs.astype(jnp.float32) * factor).astype(jnp.bfloat16)
    local_state = jnp.einsum(
        "cqgjp,cqgn->cgjpn", weighted, bs, preferred_element_type=jnp.float32
    ).reshape(blocks, heads_dev, HEAD_DIM, STATE)
    step_a = jnp.where(first[:, None], 0.0, grow)
    step_b = local_state + jnp.where(
        first[:, None, None, None], grow[:, :, None, None] * bank_state, 0.0
    )
    core = place % 2
    chip = place // 2
    chips = devices // 2
    half = heads_dev // 2
    rows = blocks * half

    def keep(part, at):
        piece = lax.dynamic_slice_in_dim(part, at * half, half, axis=1)
        return piece.reshape((rows,) + part.shape[2:])

    pair = [(source, source ^ 1) for source in range(devices)]
    mine = (keep(step_a, core), keep(step_b, core))
    got = lax.ppermute((keep(step_a, 1 - core), keep(step_b, 1 - core)), "seq", pair)
    early = jax.tree.map(lambda own, other: jnp.where(core == 0, own, other), mine, got)
    later = jax.tree.map(lambda own, other: jnp.where(core == 0, other, own), mine, got)
    run_a, run_b = combine(early, later)
    prior_a, prior_b = jnp.ones_like(run_a), jnp.zeros_like(run_b)

    def wrap(part, neutral, late):
        moved = jnp.concatenate([jnp.full_like(part[:half], neutral), part[: rows - half]], axis=0)
        return jnp.where(late, part, moved)

    span = 1
    while span < chips:
        got_a, got_b = from_behind((run_a, run_b), "seq", 2 * span)
        late = chip >= span
        lead = (wrap(got_a, 1.0, late), wrap(got_b, 0.0, late))
        run_a, run_b = combine(lead, (run_a, run_b))
        prior_a, prior_b = combine(lead, (prior_a, prior_b))
        span *= 2
    lift = combine((run_a[:half], run_b[:half]), (prior_a[half:], prior_b[half:]))[1]
    before_chip = jnp.concatenate([prior_b[:half], lift], axis=0)
    after_early = early[0][:, None, None] * before_chip + early[1]
    own_part = jnp.where(core == 0, before_chip, after_early)
    other_part = lax.ppermute(jnp.where(core == 0, after_early, before_chip), "seq", pair)
    split_rows = lambda part: part.reshape((blocks, half) + part.shape[1:])
    own_part, other_part = split_rows(own_part), split_rows(other_part)
    previous = jnp.where(
        core == 0,
        jnp.concatenate([own_part, other_part], axis=1),
        jnp.concatenate([other_part, own_part], axis=1),
    )
    state_in = jnp.where(first[:, None, None, None], bank_state, previous)
    read = jnp.einsum(
        "cqgn,cgjpn->cqgjp",
        cq.astype(jnp.float32),
        state_in.reshape(blocks, groups_dev, per_group, HEAD_DIM, STATE),
        precision=lax.Precision.HIGHEST,
    )
    growth = jnp.exp(cum).reshape(blocks, BLOCK, groups_dev, per_group, 1)
    skip = d_skip.reshape(1, 1, groups_dev, per_group, 1)
    y_total = y_intra + growth * read + skip * xs.astype(jnp.float32)
    gated = y_total.reshape(rows_dev, inner_dev) * jax.nn.silu(gate.astype(jnp.float32))
    grouped = gated.reshape(rows_dev, groups_dev, inner_dev // groups_dev)
    scale = lax.rsqrt(jnp.mean(grouped * grouped, axis=2, keepdims=True) + 1e-05)
    result = (grouped * scale).reshape(rows_dev, inner_dev) * norm_gain[None, :]
    return result.astype(jnp.bfloat16)


def solution(mesh):
    placed = (
        P("seq", "mp"),
        P(None, None, "mp"),
        P(None, None, "mp"),
        P(None, "mp"),
        P(None, "mp"),
        P("mp"),
        P(None, None, "mp"),
        P(None, "mp"),
        P("mp"),
        P("mp"),
        P("mp"),
        P("mp"),
        P(None, "mp", None, None),
        P(None, None, "mp"),
        P(None, None, None, "mp"),
        P(),
        P(),
        P(),
    )
    return jax.shard_map(
        per_device, mesh=mesh, in_specs=placed, out_specs=P("seq", "mp"), check_vma=False
    )
```

```python
import jax
import jax.numpy as jnp
from jax import lax
from jax.sharding import PartitionSpec as P

WIDTH = 4096
HEAD_DIM = 64
STATE = 128
BLOCK = 256
KERNEL = 4
BANK = 2


def from_behind(value, axis, steps):
    count = lax.axis_size(axis)
    pairs = [(source, (source + steps) % count) for source in range(count)]
    return lax.ppermute(value, axis, pairs)


def combine(earlier, later):
    return (earlier[0] * later[0], later[0][:, None, None] * earlier[1] + later[1])


def per_device(
    hidden,
    w_zx,
    w_bc,
    w_dt,
    conv_x,
    conv_x_bias,
    conv_bc,
    conv_bc_bias,
    a_log,
    dt_bias,
    d_skip,
    norm_gain,
    state_bank,
    conv_bank_x,
    conv_bank_bc,
    prompt_blocks,
    prompt_order,
    resume_slot,
):
    devices = lax.axis_size("seq")
    place = lax.axis_index("seq")
    rows_dev = hidden.shape[0]
    blocks = rows_dev // BLOCK
    inner_dev = w_zx.shape[2]
    gstate_dev = w_bc.shape[2]
    heads_dev = w_dt.shape[1]
    groups_dev = gstate_dev // STATE
    per_group = heads_dev // groups_dev
    channels = inner_dev + 2 * gstate_dev
    prompts = prompt_blocks.shape[0]
    flat_zx = w_zx.reshape(WIDTH, 2 * inner_dev)
    flat_bc = w_bc.reshape(WIDTH, 2 * gstate_dev)
    piece = lax.all_gather(hidden, "mp", axis=1, tiled=True)
    zx_sum = jnp.dot(piece, flat_zx, preferred_element_type=jnp.float32)
    bc_sum = jnp.dot(piece, flat_bc, preferred_element_type=jnp.float32)
    dt_raw = jnp.dot(piece, w_dt, preferred_element_type=jnp.float32)
    zx = zx_sum.astype(jnp.bfloat16)
    bc = bc_sum.astype(jnp.bfloat16)
    gate = zx[:, :inner_dev]
    mixin = jnp.concatenate([zx[:, inner_dev:], bc], axis=1).reshape(blocks, BLOCK, channels)
    own_tails = mixin[:, BLOCK - (KERNEL - 1) :, :]
    arrived = from_behind(own_tails, "seq", 1)
    wrapped = jnp.concatenate([jnp.zeros_like(arrived[:1]), arrived[:-1]], axis=0)
    before = jnp.where(place > 0, arrived, wrapped)
    prompt_ids = jnp.arange(prompts, dtype=jnp.int32)
    order_hot = (prompt_order[:, None] == prompt_ids[None, :]).astype(jnp.int32)
    lengths = jnp.sum(order_hot * prompt_blocks[None, :], axis=1)
    slots = jnp.sum(order_hot * resume_slot[None, :], axis=1)
    ends = jnp.cumsum(lengths)
    starts = ends - lengths
    stream_ids = jnp.arange(blocks, dtype=jnp.int32) * devices + place
    inside = (
        (stream_ids[:, None] >= starts[None, :]) & (stream_ids[:, None] < ends[None, :])
    ).astype(jnp.int32)
    block_slot = jnp.sum(inside * slots[None, :], axis=1)
    first = jnp.any(stream_ids[:, None] == starts[None, :], axis=1)
    pick = (block_slot[:, None] == jnp.arange(BANK, dtype=jnp.int32)[None, :]).astype(jnp.float32)
    bank_state = jnp.einsum("cr,rhpn->chpn", pick, state_bank, precision=lax.Precision.HIGHEST)
    bank_rows = jnp.concatenate(
        [conv_bank_x, conv_bank_bc.reshape(BANK, KERNEL - 1, 2 * gstate_dev)], axis=2
    )
    bank_tail = jnp.einsum("cr,rkz->ckz", pick, bank_rows.astype(jnp.float32)).astype(jnp.bfloat16)
    tail = jnp.where(first[:, None, None], bank_tail, before)
    kernel = jnp.concatenate([conv_x, conv_bc.reshape(KERNEL, 2 * gstate_dev)], axis=1)
    bias = jnp.concatenate([conv_x_bias, conv_bc_bias.reshape(2 * gstate_dev)], axis=0)
    padded = jnp.concatenate([tail, mixin], axis=1).astype(jnp.float32)
    acc = bias[None, None, :] + padded[:, 0:BLOCK] * kernel[0]
    for k in range(1, KERNEL):
        acc = acc + padded[:, k : k + BLOCK] * kernel[k]
    conv = jax.nn.silu(acc).astype(jnp.bfloat16)
    xs = conv[..., :inner_dev].reshape(blocks, BLOCK, groups_dev, per_group, HEAD_DIM)
    bs = conv[..., inner_dev : inner_dev + gstate_dev].reshape(blocks, BLOCK, groups_dev, STATE)
    cq = conv[..., inner_dev + gstate_dev :].reshape(blocks, BLOCK, groups_dev, STATE)
    dt = jax.nn.softplus(dt_raw.reshape(blocks, BLOCK, heads_dev) + dt_bias[None, None, :])
    cum = jnp.cumsum(dt * (-jnp.exp(a_log))[None, None, :], axis=1)
    scores = jnp.einsum("cqgn,ckgn->cgqk", cq, bs, preferred_element_type=jnp.float32)
    cum_h = cum.transpose(0, 2, 1)
    lower = jnp.arange(BLOCK)[:, None] >= jnp.arange(BLOCK)[None, :]
    damp = jnp.exp(
        jnp.where(lower[None, None], cum_h[:, :, :, None] - cum_h[:, :, None, :], -jnp.inf)
    )
    damp = damp.reshape(blocks, groups_dev, per_group, BLOCK, BLOCK)
    dt_h = dt.transpose(0, 2, 1).reshape(blocks, groups_dev, per_group, 1, BLOCK)
    mix = (scores[:, :, None] * damp * dt_h).astype(jnp.bfloat16)
    y_intra = jnp.einsum("cgjqk,ckgjp->cqgjp", mix, xs, preferred_element_type=jnp.float32)
    last = cum[:, -1, :]
    grow = jnp.exp(last)
    factor = (dt * jnp.exp(last[:, None, :] - cum)).reshape(blocks, BLOCK, groups_dev, per_group, 1)
    weighted = (xs.astype(jnp.float32) * factor).astype(jnp.bfloat16)
    local_state = jnp.einsum(
        "cqgjp,cqgn->cgjpn", weighted, bs, preferred_element_type=jnp.float32
    ).reshape(blocks, heads_dev, HEAD_DIM, STATE)
    step_a = jnp.where(first[:, None], 0.0, grow)
    step_b = local_state + jnp.where(
        first[:, None, None, None], grow[:, :, None, None] * bank_state, 0.0
    )
    core = place % 2
    chip = place // 2
    chips = devices // 2
    half = heads_dev // 2
    rows = blocks * half

    def keep(part, at):
        piece = lax.dynamic_slice_in_dim(part, at * half, half, axis=1)
        return piece.reshape((rows,) + part.shape[2:])

    pair = [(source, source ^ 1) for source in range(devices)]
    mine = (keep(step_a, core), keep(step_b, core))
    got = lax.ppermute((keep(step_a, 1 - core), keep(step_b, 1 - core)), "seq", pair)
    early = jax.tree.map(lambda own, other: jnp.where(core == 0, own, other), mine, got)
    later = jax.tree.map(lambda own, other: jnp.where(core == 0, other, own), mine, got)
    quarter = half // 2
    split_heads = lambda part: [
        part.reshape((blocks, 2, quarter) + part.shape[1:])[:, g].reshape((blocks * quarter,) + part.shape[1:])
        for g in range(2)
    ]
    chip_a, chip_b = combine(early, later)
    lanes = [list(pair) for pair in zip(split_heads(chip_a), split_heads(chip_b))]
    priors = [[jnp.ones_like(lane[0]), jnp.zeros_like(lane[1])] for lane in lanes]

    def wrap(part, neutral, late):
        moved = jnp.concatenate([jnp.full_like(part[:quarter], neutral), part[: part.shape[0] - quarter]], axis=0)
        return jnp.where(late, part, moved)

    span = 1
    while span < chips:
        late = chip >= span
        for g in range(2):
            got_a, got_b = from_behind(tuple(lanes[g]), "seq", 2 * span)
            lead = (wrap(got_a, 1.0, late), wrap(got_b, 0.0, late))
            lanes[g] = list(combine(lead, tuple(lanes[g])))
            priors[g] = list(combine(lead, tuple(priors[g])))
        span *= 2
    joined = []
    for g in range(2):
        run_a, run_b = lanes[g]
        prior_a, prior_b = priors[g]
        lift = combine((run_a[:quarter], run_b[:quarter]), (prior_a[quarter:], prior_b[quarter:]))[1]
        joined.append(jnp.concatenate([prior_b[:quarter], lift], axis=0))
    before_chip = jnp.concatenate(
        [part.reshape((blocks, quarter) + part.shape[1:]) for part in joined], axis=1
    ).reshape(chip_b.shape)
    after_early = early[0][:, None, None] * before_chip + early[1]
    own_part = jnp.where(core == 0, before_chip, after_early)
    other_part = lax.ppermute(jnp.where(core == 0, after_early, before_chip), "seq", pair)
    split_rows = lambda part: part.reshape((blocks, half) + part.shape[1:])
    own_part, other_part = split_rows(own_part), split_rows(other_part)
    previous = jnp.where(
        core == 0,
        jnp.concatenate([own_part, other_part], axis=1),
        jnp.concatenate([other_part, own_part], axis=1),
    )
    state_in = jnp.where(first[:, None, None, None], bank_state, previous)
    read = jnp.einsum(
        "cqgn,cgjpn->cqgjp",
        cq.astype(jnp.float32),
        state_in.reshape(blocks, groups_dev, per_group, HEAD_DIM, STATE),
        precision=lax.Precision.HIGHEST,
    )
    growth = jnp.exp(cum).reshape(blocks, BLOCK, groups_dev, per_group, 1)
    skip = d_skip.reshape(1, 1, groups_dev, per_group, 1)
    y_total = y_intra + growth * read + skip * xs.astype(jnp.float32)
    gated = y_total.reshape(rows_dev, inner_dev) * jax.nn.silu(gate.astype(jnp.float32))
    grouped = gated.reshape(rows_dev, groups_dev, inner_dev // groups_dev)
    scale = lax.rsqrt(jnp.mean(grouped * grouped, axis=2, keepdims=True) + 1e-05)
    result = (grouped * scale).reshape(rows_dev, inner_dev) * norm_gain[None, :]
    return result.astype(jnp.bfloat16)


def solution(mesh):
    placed = (
        P("seq", "mp"),
        P(None, None, "mp"),
        P(None, None, "mp"),
        P(None, "mp"),
        P(None, "mp"),
        P("mp"),
        P(None, None, "mp"),
        P(None, "mp"),
        P("mp"),
        P("mp"),
        P("mp"),
        P("mp"),
        P(None, "mp", None, None),
        P(None, None, "mp"),
        P(None, None, None, "mp"),
        P(),
        P(),
        P(),
    )
    return jax.shard_map(
        per_device, mesh=mesh, in_specs=placed, out_specs=P("seq", "mp"), check_vma=False
    )
```

```python
import jax
import jax.numpy as jnp
from jax import lax
from jax.sharding import PartitionSpec as P

WIDTH = 4096
HEAD_DIM = 64
STATE = 128
BLOCK = 256
KERNEL = 4
BANK = 2
SCAN_BANDS = 4


def from_behind(value, axis, steps):
    count = lax.axis_size(axis)
    pairs = [(source, (source + steps) % count) for source in range(count)]
    return lax.ppermute(value, axis, pairs)


def combine(earlier, later):
    return (earlier[0] * later[0], later[0][:, None, None] * earlier[1] + later[1])


def per_device(
    hidden,
    w_zx,
    w_bc,
    w_dt,
    conv_x,
    conv_x_bias,
    conv_bc,
    conv_bc_bias,
    a_log,
    dt_bias,
    d_skip,
    norm_gain,
    state_bank,
    conv_bank_x,
    conv_bank_bc,
    prompt_blocks,
    prompt_order,
    resume_slot,
):
    devices = lax.axis_size("seq")
    place = lax.axis_index("seq")
    rows_dev = hidden.shape[0]
    blocks = rows_dev // BLOCK
    inner_dev = w_zx.shape[2]
    gstate_dev = w_bc.shape[2]
    heads_dev = w_dt.shape[1]
    groups_dev = gstate_dev // STATE
    per_group = heads_dev // groups_dev
    channels = inner_dev + 2 * gstate_dev
    prompts = prompt_blocks.shape[0]
    flat_zx = w_zx.reshape(WIDTH, 2 * inner_dev)
    flat_bc = w_bc.reshape(WIDTH, 2 * gstate_dev)
    piece = lax.all_gather(hidden, "mp", axis=1, tiled=True)
    zx_sum = jnp.dot(piece, flat_zx, preferred_element_type=jnp.float32)
    bc_sum = jnp.dot(piece, flat_bc, preferred_element_type=jnp.float32)
    dt_raw = jnp.dot(piece, w_dt, preferred_element_type=jnp.float32)
    zx = zx_sum.astype(jnp.bfloat16)
    bc = bc_sum.astype(jnp.bfloat16)
    gate = zx[:, :inner_dev]
    mixin = jnp.concatenate([zx[:, inner_dev:], bc], axis=1).reshape(blocks, BLOCK, channels)
    own_tails = mixin[:, BLOCK - (KERNEL - 1) :, :]
    arrived = from_behind(own_tails, "seq", 1)
    wrapped = jnp.concatenate([jnp.zeros_like(arrived[:1]), arrived[:-1]], axis=0)
    before = jnp.where(place > 0, arrived, wrapped)
    prompt_ids = jnp.arange(prompts, dtype=jnp.int32)
    order_hot = (prompt_order[:, None] == prompt_ids[None, :]).astype(jnp.int32)
    lengths = jnp.sum(order_hot * prompt_blocks[None, :], axis=1)
    slots = jnp.sum(order_hot * resume_slot[None, :], axis=1)
    ends = jnp.cumsum(lengths)
    starts = ends - lengths
    stream_ids = jnp.arange(blocks, dtype=jnp.int32) * devices + place
    inside = (
        (stream_ids[:, None] >= starts[None, :]) & (stream_ids[:, None] < ends[None, :])
    ).astype(jnp.int32)
    block_slot = jnp.sum(inside * slots[None, :], axis=1)
    first = jnp.any(stream_ids[:, None] == starts[None, :], axis=1)
    pick = (block_slot[:, None] == jnp.arange(BANK, dtype=jnp.int32)[None, :]).astype(jnp.float32)
    bank_state = jnp.einsum("cr,rhpn->chpn", pick, state_bank, precision=lax.Precision.HIGHEST)
    bank_rows = jnp.concatenate(
        [conv_bank_x, conv_bank_bc.reshape(BANK, KERNEL - 1, 2 * gstate_dev)], axis=2
    )
    bank_tail = jnp.einsum("cr,rkz->ckz", pick, bank_rows.astype(jnp.float32)).astype(jnp.bfloat16)
    tail = jnp.where(first[:, None, None], bank_tail, before)
    kernel = jnp.concatenate([conv_x, conv_bc.reshape(KERNEL, 2 * gstate_dev)], axis=1)
    bias = jnp.concatenate([conv_x_bias, conv_bc_bias.reshape(2 * gstate_dev)], axis=0)
    padded = jnp.concatenate([tail, mixin], axis=1).astype(jnp.float32)
    acc = bias[None, None, :] + padded[:, 0:BLOCK] * kernel[0]
    for k in range(1, KERNEL):
        acc = acc + padded[:, k : k + BLOCK] * kernel[k]
    conv = jax.nn.silu(acc).astype(jnp.bfloat16)
    xs = conv[..., :inner_dev].reshape(blocks, BLOCK, groups_dev, per_group, HEAD_DIM)
    bs = conv[..., inner_dev : inner_dev + gstate_dev].reshape(blocks, BLOCK, groups_dev, STATE)
    cq = conv[..., inner_dev + gstate_dev :].reshape(blocks, BLOCK, groups_dev, STATE)
    dt = jax.nn.softplus(dt_raw.reshape(blocks, BLOCK, heads_dev) + dt_bias[None, None, :])
    cum = jnp.cumsum(dt * (-jnp.exp(a_log))[None, None, :], axis=1)
    scores = jnp.einsum("cqgn,ckgn->cgqk", cq, bs, preferred_element_type=jnp.float32)
    cum_h = cum.transpose(0, 2, 1)
    lower = jnp.arange(BLOCK)[:, None] >= jnp.arange(BLOCK)[None, :]
    damp = jnp.exp(
        jnp.where(lower[None, None], cum_h[:, :, :, None] - cum_h[:, :, None, :], -jnp.inf)
    )
    damp = damp.reshape(blocks, groups_dev, per_group, BLOCK, BLOCK)
    dt_h = dt.transpose(0, 2, 1).reshape(blocks, groups_dev, per_group, 1, BLOCK)
    mix = (scores[:, :, None] * damp * dt_h).astype(jnp.bfloat16)
    y_intra = jnp.einsum("cgjqk,ckgjp->cqgjp", mix, xs, preferred_element_type=jnp.float32)
    last = cum[:, -1, :]
    grow = jnp.exp(last)
    factor = (dt * jnp.exp(last[:, None, :] - cum)).reshape(blocks, BLOCK, groups_dev, per_group, 1)
    weighted = (xs.astype(jnp.float32) * factor).astype(jnp.bfloat16)
    local_state = jnp.einsum(
        "cqgjp,cqgn->cgjpn", weighted, bs, preferred_element_type=jnp.float32
    ).reshape(blocks, heads_dev, HEAD_DIM, STATE)
    step_a = jnp.where(first[:, None], 0.0, grow)
    step_b = local_state + jnp.where(
        first[:, None, None, None], grow[:, :, None, None] * bank_state, 0.0
    )
    core = place % 2
    chip = place // 2
    chips = devices // 2
    half = heads_dev // 2
    rows = blocks * half

    def keep(part, at):
        piece = lax.dynamic_slice_in_dim(part, at * half, half, axis=1)
        return piece.reshape((rows,) + part.shape[2:])

    pair = [(source, source ^ 1) for source in range(devices)]
    mine = (keep(step_a, core), keep(step_b, core))
    got = lax.ppermute((keep(step_a, 1 - core), keep(step_b, 1 - core)), "seq", pair)
    early = jax.tree.map(lambda own, other: jnp.where(core == 0, own, other), mine, got)
    later = jax.tree.map(lambda own, other: jnp.where(core == 0, other, own), mine, got)
    bands = SCAN_BANDS
    quarter = half // bands
    split_heads = lambda part: [
        part.reshape((blocks, bands, quarter) + part.shape[1:])[:, g].reshape((blocks * quarter,) + part.shape[1:])
        for g in range(bands)
    ]
    chip_a, chip_b = combine(early, later)
    lanes = [list(pair) for pair in zip(split_heads(chip_a), split_heads(chip_b))]
    priors = [[jnp.ones_like(lane[0]), jnp.zeros_like(lane[1])] for lane in lanes]

    def wrap(part, neutral, late):
        moved = jnp.concatenate([jnp.full_like(part[:quarter], neutral), part[: part.shape[0] - quarter]], axis=0)
        return jnp.where(late, part, moved)

    span = 1
    while span < chips:
        late = chip >= span
        for g in range(bands):
            got_a, got_b = from_behind(tuple(lanes[g]), "seq", 2 * span)
            lead = (wrap(got_a, 1.0, late), wrap(got_b, 0.0, late))
            lanes[g] = list(combine(lead, tuple(lanes[g])))
            priors[g] = list(combine(lead, tuple(priors[g])))
        span *= 2
    joined = []
    for g in range(bands):
        run_a, run_b = lanes[g]
        prior_a, prior_b = priors[g]
        lift = combine((run_a[:quarter], run_b[:quarter]), (prior_a[quarter:], prior_b[quarter:]))[1]
        joined.append(jnp.concatenate([prior_b[:quarter], lift], axis=0))
    before_chip = jnp.concatenate(
        [part.reshape((blocks, quarter) + part.shape[1:]) for part in joined], axis=1
    ).reshape(chip_b.shape)
    after_early = early[0][:, None, None] * before_chip + early[1]
    own_part = jnp.where(core == 0, before_chip, after_early)
    other_part = lax.ppermute(jnp.where(core == 0, after_early, before_chip), "seq", pair)
    split_rows = lambda part: part.reshape((blocks, half) + part.shape[1:])
    own_part, other_part = split_rows(own_part), split_rows(other_part)
    previous = jnp.where(
        core == 0,
        jnp.concatenate([own_part, other_part], axis=1),
        jnp.concatenate([other_part, own_part], axis=1),
    )
    state_in = jnp.where(first[:, None, None, None], bank_state, previous)
    read = jnp.einsum(
        "cqgn,cgjpn->cqgjp",
        cq.astype(jnp.float32),
        state_in.reshape(blocks, groups_dev, per_group, HEAD_DIM, STATE),
        precision=lax.Precision.HIGHEST,
    )
    growth = jnp.exp(cum).reshape(blocks, BLOCK, groups_dev, per_group, 1)
    skip = d_skip.reshape(1, 1, groups_dev, per_group, 1)
    y_total = y_intra + growth * read + skip * xs.astype(jnp.float32)
    gated = y_total.reshape(rows_dev, inner_dev) * jax.nn.silu(gate.astype(jnp.float32))
    grouped = gated.reshape(rows_dev, groups_dev, inner_dev // groups_dev)
    scale = lax.rsqrt(jnp.mean(grouped * grouped, axis=2, keepdims=True) + 1e-05)
    result = (grouped * scale).reshape(rows_dev, inner_dev) * norm_gain[None, :]
    return result.astype(jnp.bfloat16)


def solution(mesh):
    placed = (
        P("seq", "mp"),
        P(None, None, "mp"),
        P(None, None, "mp"),
        P(None, "mp"),
        P(None, "mp"),
        P("mp"),
        P(None, None, "mp"),
        P(None, "mp"),
        P("mp"),
        P("mp"),
        P("mp"),
        P("mp"),
        P(None, "mp", None, None),
        P(None, None, "mp"),
        P(None, None, None, "mp"),
        P(),
        P(),
        P(),
    )
    return jax.shard_map(
        per_device, mesh=mesh, in_specs=placed, out_specs=P("seq", "mp"), check_vma=False
    )
```

```python
import jax
import jax.numpy as jnp
from jax import lax
from jax.sharding import PartitionSpec as P

WIDTH = 4096
HEAD_DIM = 64
STATE = 128
BLOCK = 256
KERNEL = 4
BANK = 2


def from_behind(value, axis, steps):
    count = lax.axis_size(axis)
    pairs = [(source, (source + steps) % count) for source in range(count)]
    return lax.ppermute(value, axis, pairs)


def combine(earlier, later):
    return (earlier[0] * later[0], later[0][:, None, None] * earlier[1] + later[1])


def per_device(
    hidden,
    w_zx,
    w_bc,
    w_dt,
    conv_x,
    conv_x_bias,
    conv_bc,
    conv_bc_bias,
    a_log,
    dt_bias,
    d_skip,
    norm_gain,
    state_bank,
    conv_bank_x,
    conv_bank_bc,
    prompt_blocks,
    prompt_order,
    resume_slot,
):
    devices = lax.axis_size("seq")
    place = lax.axis_index("seq")
    rows_dev = hidden.shape[0]
    blocks = rows_dev // BLOCK
    inner_dev = w_zx.shape[2]
    gstate_dev = w_bc.shape[2]
    heads_dev = w_dt.shape[1]
    groups_dev = gstate_dev // STATE
    per_group = heads_dev // groups_dev
    channels = inner_dev + 2 * gstate_dev
    prompts = prompt_blocks.shape[0]
    flat_zx = w_zx.reshape(WIDTH, 2 * inner_dev)
    flat_bc = w_bc.reshape(WIDTH, 2 * gstate_dev)
    piece = lax.all_gather(hidden, "mp", axis=1, tiled=True)
    zx_sum = jnp.dot(piece, flat_zx, preferred_element_type=jnp.float32)
    bc_sum = jnp.dot(piece, flat_bc, preferred_element_type=jnp.float32)
    dt_raw = jnp.dot(piece, w_dt, preferred_element_type=jnp.float32)
    zx = zx_sum.astype(jnp.bfloat16)
    bc = bc_sum.astype(jnp.bfloat16)
    gate = zx[:, :inner_dev]
    mixin = jnp.concatenate([zx[:, inner_dev:], bc], axis=1).reshape(blocks, BLOCK, channels)
    own_tails = mixin[:, BLOCK - (KERNEL - 1) :, :]
    arrived = from_behind(own_tails, "seq", 1)
    wrapped = jnp.concatenate([jnp.zeros_like(arrived[:1]), arrived[:-1]], axis=0)
    before = jnp.where(place > 0, arrived, wrapped)
    prompt_ids = jnp.arange(prompts, dtype=jnp.int32)
    order_hot = (prompt_order[:, None] == prompt_ids[None, :]).astype(jnp.int32)
    lengths = jnp.sum(order_hot * prompt_blocks[None, :], axis=1)
    slots = jnp.sum(order_hot * resume_slot[None, :], axis=1)
    ends = jnp.cumsum(lengths)
    starts = ends - lengths
    stream_ids = jnp.arange(blocks, dtype=jnp.int32) * devices + place
    inside = (
        (stream_ids[:, None] >= starts[None, :]) & (stream_ids[:, None] < ends[None, :])
    ).astype(jnp.int32)
    block_slot = jnp.sum(inside * slots[None, :], axis=1)
    first = jnp.any(stream_ids[:, None] == starts[None, :], axis=1)
    pick = (block_slot[:, None] == jnp.arange(BANK, dtype=jnp.int32)[None, :]).astype(jnp.float32)
    bank_state = jnp.einsum("cr,rhpn->chpn", pick, state_bank, precision=lax.Precision.HIGHEST)
    bank_rows = jnp.concatenate(
        [conv_bank_x, conv_bank_bc.reshape(BANK, KERNEL - 1, 2 * gstate_dev)], axis=2
    )
    bank_tail = jnp.einsum("cr,rkz->ckz", pick, bank_rows.astype(jnp.float32)).astype(jnp.bfloat16)
    tail = jnp.where(first[:, None, None], bank_tail, before)
    kernel = jnp.concatenate([conv_x, conv_bc.reshape(KERNEL, 2 * gstate_dev)], axis=1)
    bias = jnp.concatenate([conv_x_bias, conv_bc_bias.reshape(2 * gstate_dev)], axis=0)
    padded = jnp.concatenate([tail, mixin], axis=1).astype(jnp.float32)
    acc = bias[None, None, :] + padded[:, 0:BLOCK] * kernel[0]
    for k in range(1, KERNEL):
        acc = acc + padded[:, k : k + BLOCK] * kernel[k]
    conv = jax.nn.silu(acc).astype(jnp.bfloat16)
    xs = conv[..., :inner_dev].reshape(blocks, BLOCK, groups_dev, per_group, HEAD_DIM)
    bs = conv[..., inner_dev : inner_dev + gstate_dev].reshape(blocks, BLOCK, groups_dev, STATE)
    cq = conv[..., inner_dev + gstate_dev :].reshape(blocks, BLOCK, groups_dev, STATE)
    dt = jax.nn.softplus(dt_raw.reshape(blocks, BLOCK, heads_dev) + dt_bias[None, None, :])
    cum = jnp.cumsum(dt * (-jnp.exp(a_log))[None, None, :], axis=1)
    scores = jnp.einsum("cqgn,ckgn->cgqk", cq, bs, preferred_element_type=jnp.float32)
    cum_h = cum.transpose(0, 2, 1)
    lower = jnp.arange(BLOCK)[:, None] >= jnp.arange(BLOCK)[None, :]
    damp = jnp.exp(
        jnp.where(lower[None, None], cum_h[:, :, :, None] - cum_h[:, :, None, :], -jnp.inf)
    )
    damp = damp.reshape(blocks, groups_dev, per_group, BLOCK, BLOCK)
    dt_h = dt.transpose(0, 2, 1).reshape(blocks, groups_dev, per_group, 1, BLOCK)
    mix = (scores[:, :, None] * damp * dt_h).astype(jnp.bfloat16)
    y_intra = jnp.einsum("cgjqk,ckgjp->cqgjp", mix, xs, preferred_element_type=jnp.float32)
    last = cum[:, -1, :]
    grow = jnp.exp(last)
    factor = (dt * jnp.exp(last[:, None, :] - cum)).reshape(blocks, BLOCK, groups_dev, per_group, 1)
    weighted = (xs.astype(jnp.float32) * factor).astype(jnp.bfloat16)
    local_state = jnp.einsum(
        "cqgjp,cqgn->cgjpn", weighted, bs, preferred_element_type=jnp.float32
    ).reshape(blocks, heads_dev, HEAD_DIM, STATE)
    step_a = jnp.where(first[:, None], 0.0, grow)
    step_b = local_state + jnp.where(
        first[:, None, None, None], grow[:, :, None, None] * bank_state, 0.0
    )
    core = place % 2
    chip = place // 2
    chips = devices // 2
    half = heads_dev // 2
    rows = blocks * half

    def keep(part, at):
        piece = lax.dynamic_slice_in_dim(part, at * half, half, axis=1)
        return piece.reshape((rows,) + part.shape[2:])

    pair = [(source, source ^ 1) for source in range(devices)]
    mine = (keep(step_a, core), keep(step_b, core))
    got = lax.ppermute((keep(step_a, 1 - core), keep(step_b, 1 - core)), "seq", pair)
    early = jax.tree.map(lambda own, other: jnp.where(core == 0, own, other), mine, got)
    later = jax.tree.map(lambda own, other: jnp.where(core == 0, other, own), mine, got)
    quarter = half // 2
    split_heads = lambda part: [
        part.reshape((blocks, 2, quarter) + part.shape[1:])[:, g].reshape((blocks * quarter,) + part.shape[1:])
        for g in range(2)
    ]
    chip_a, chip_b = combine(early, later)
    lanes = [list(pair) for pair in zip(split_heads(chip_a), split_heads(chip_b))]
    priors = [[jnp.ones_like(lane[0]), jnp.zeros_like(lane[1])] for lane in lanes]

    def wrap(part, neutral, late):
        moved = jnp.concatenate([jnp.full_like(part[:quarter], neutral), part[: part.shape[0] - quarter]], axis=0)
        return jnp.where(late, part, moved)

    span = 1
    while span < chips:
        late = chip >= span
        for g in range(2):
            got_a, got_b = from_behind(tuple(lanes[g]), "seq", 2 * span)
            lead = (wrap(got_a, 1.0, late), wrap(got_b, 0.0, late))
            lanes[g] = list(combine(lead, tuple(lanes[g])))
            priors[g] = list(combine(lead, tuple(priors[g])))
        span *= 2
    joined = []
    for g in range(2):
        run_a, run_b = lanes[g]
        prior_a, prior_b = priors[g]
        lift = combine((run_a[:quarter], run_b[:quarter]), (prior_a[quarter:], prior_b[quarter:]))[1]
        joined.append(jnp.concatenate([prior_b[:quarter], lift], axis=0))
    before_chip = jnp.concatenate(
        [part.reshape((blocks, quarter) + part.shape[1:]) for part in joined], axis=1
    ).reshape(chip_b.shape)
    after_early = early[0][:, None, None] * before_chip + early[1]
    own_part = jnp.where(core == 0, before_chip, after_early)
    other_part = lax.ppermute(jnp.where(core == 0, after_early, before_chip), "seq", pair)
    previous = []
    for r in range(blocks):
        own_r, other_r = own_part[r * half : (r + 1) * half], other_part[r * half : (r + 1) * half]
        previous.append(jnp.where(core == 0, jnp.concatenate([own_r, other_r]), jnp.concatenate([other_r, own_r])))
    previous = jnp.stack(previous)
    state_in = jnp.where(first[:, None, None, None], bank_state, previous)
    read = jnp.einsum(
        "cqgn,cgjpn->cqgjp",
        cq.astype(jnp.float32),
        state_in.reshape(blocks, groups_dev, per_group, HEAD_DIM, STATE),
        precision=lax.Precision.HIGHEST,
    )
    growth = jnp.exp(cum).reshape(blocks, BLOCK, groups_dev, per_group, 1)
    skip = d_skip.reshape(1, 1, groups_dev, per_group, 1)
    y_total = y_intra + growth * read + skip * xs.astype(jnp.float32)
    gated = y_total.reshape(rows_dev, inner_dev) * jax.nn.silu(gate.astype(jnp.float32))
    grouped = gated.reshape(rows_dev, groups_dev, inner_dev // groups_dev)
    scale = lax.rsqrt(jnp.mean(grouped * grouped, axis=2, keepdims=True) + 1e-05)
    result = (grouped * scale).reshape(rows_dev, inner_dev) * norm_gain[None, :]
    return result.astype(jnp.bfloat16)


def solution(mesh):
    placed = (
        P("seq", "mp"),
        P(None, None, "mp"),
        P(None, None, "mp"),
        P(None, "mp"),
        P(None, "mp"),
        P("mp"),
        P(None, None, "mp"),
        P(None, "mp"),
        P("mp"),
        P("mp"),
        P("mp"),
        P("mp"),
        P(None, "mp", None, None),
        P(None, None, "mp"),
        P(None, None, None, "mp"),
        P(),
        P(),
        P(),
    )
    return jax.shard_map(
        per_device, mesh=mesh, in_specs=placed, out_specs=P("seq", "mp"), check_vma=False
    )
```
